256 devices in a mesh: blk: 32 (over z, y), group: 8 (over x, core).
Axes of the slice: x: 4, y: 4, z: 8, core: 2. Of those that a mesh axis runs over, the one named last changes fastest.
Arguments:
- queries: bfloat16 [32, 2048, 2560], P('blk', 'group'), may hold values from -16 to 16
- new_kv: bfloat16 [32, 2048, 512], P('blk', 'group'), may hold values from -16 to 16
- kv_pool: bfloat16 [1024, 128, 512], P('blk'), may hold values from -16 to 16
- window_table: int32 [32, 16], replicated, may hold values from 0 to 1023, as said below
- append_table: int32 [32, 16], replicated, may hold values from 0 to 1023, as said below
- cache_lengths: int32 [32], replicated, may hold values from 0 to 16384, as said below
Outputs:
- attn_out: bfloat16 [32, 2048, 2560], P('blk', 'group')
- new_pool: bfloat16 [1024, 128, 512], P('blk')
The draws below stay inside these ranges and needn't reach their ends.
Inputs may be any that keep to these rules, and one draw needn't show every extreme that they name: `window_table`: pool page p lies on blk index p // 32. The two tables together name every pool page exactly once. For each k, each blk index holds window page k of exactly one request; at most 1 window pages of one request lie on one blk index, and some request has that many there. `append_table`: for each k, each blk index receives appended page k of exactly one request; at most one appended page of one request goes to one blk index, and some request sends one there. `cache_lengths`: A multiple of 128; some request has no cached token and some has 16384.
All inputs are finite; a program needn't handle non-finite values.
Results may differ from the reference program's by a relative error of at most 0.0043.
Values may be sent and summed in bfloat16 or wider, within the bound.
No kernel may reach another device: no remote copies, remote signals or barrier semaphores. Data moves between devices by JAX's collectives and lax.ppermute only.
A program may use at most 128 MiB of HBM per device.

```python
import jax
import jax.numpy as jnp
from jax import lax

H = 10
DH = 256
W = 2048
PAGE = 128
LMAX = 16384
WP = 16
CH = 2048
NPN = 16
PB = 32
REQS = 32
POOL = 1024


def direction(key):
    flips = jax.random.bernoulli(jax.random.fold_in(key, 5), 0.5, (DH,))
    return jnp.where(flips, 1.0, -1.0).astype(jnp.float32)


def base_values(key, shape):
    first = jax.random.fold_in(key, 0)
    return jax.random.truncated_normal(first, -4.0, 4.0, shape, jnp.float32)


def key_rows(key, salt, lead_shape, row_count):
    values = base_values(jax.random.fold_in(key, salt), lead_shape + (row_count, 2 * DH))
    row_index = jnp.arange(row_count) % 23
    vector = direction(key)
    keys_part = values[..., :DH]
    keys_part = jnp.where((row_index == 5)[:, None], vector, keys_part)
    keys_part = jnp.where((row_index == 6)[:, None], 0.99 * vector, keys_part)
    return jnp.concatenate([keys_part, values[..., DH:]], axis=-1).astype(jnp.bfloat16)


def draw_queries(key, part):
    values = base_values(jax.random.fold_in(key, 31), (REQS, CH, H, DH))
    strength = 8.0 + 4.0 * (jnp.arange(H) % 3).astype(jnp.float32)
    aligned = strength[None, None, :, None] * direction(key)[None, None, None, :]
    picked = (jnp.arange(CH) % 29 == 3)[None, :, None, None]
    values = jnp.where(picked, aligned, values)
    return values.reshape(REQS, CH, H * DH).astype(jnp.bfloat16)


def draw_new_kv(key, part):
    return key_rows(key, 41, (REQS,), CH)


def draw_kv_pool(key, part):
    return key_rows(key, 43, (POOL,), PAGE)


def slot_order(sub_key):
    return jax.random.permutation(sub_key, PB)


def ordered_shifts(sub_key, count):
    total = max(count, REQS)
    candidates = jnp.arange(total) % REQS
    scores = jax.random.permutation(sub_key, total)
    scores = scores.at[1].set(total).at[REQS - 1].set(total + 1).at[REQS // 2].set(total + 2)
    order = jnp.argsort(scores)
    return candidates[order[total - count:]]


def allocate(key):
    base = jax.random.fold_in(key, 11)
    first, second, third = jax.random.split(base, 3)
    shift_win = ordered_shifts(first, WP)
    shift_new = jax.random.permutation(second, jnp.arange(max(NPN, REQS)) % REQS)[:NPN]
    orders = jax.vmap(slot_order)(jax.random.split(third, REQS))
    requests = jnp.arange(REQS)[:, None]
    owner_win = (requests + shift_win[None, :]) % REQS
    owner_new = (requests + shift_new[None, :]) % REQS
    slot_win = orders[owner_win, jnp.arange(WP)[None, :]]
    slot_new = orders[owner_new, WP + jnp.arange(NPN)[None, :]]
    return ((owner_win * PB + slot_win).astype(jnp.int32), (owner_new * PB + slot_new).astype(jnp.int32))


def draw_window_table(key, part):
    return allocate(key)[0]


def draw_append_table(key, part):
    return allocate(key)[1]


def draw_cache_lengths(key, part):
    first, second, third = jax.random.split(jax.random.fold_in(key, 23), 3)
    most = LMAX // PAGE
    pages = jnp.minimum(jax.random.randint(first, (REQS,), 0, most + 1), jax.random.randint(second, (REQS,), 0, most + 1))
    chosen = jax.random.randint(third, (), 0, REQS)
    index = jnp.arange(REQS)
    pages = jnp.where(index == chosen, most, pages)
    pages = jnp.where(index == (chosen + 1) % REQS, 0, pages)
    return (pages * PAGE).astype(jnp.int32)


def setup_inputs(seed: int = 0) -> dict:
    arg_keys = jax.random.split(jax.random.key(seed), 7)
    queries = draw_queries(jax.random.fold_in(arg_keys[6], 71), 0)
    new_kv = draw_new_kv(jax.random.fold_in(arg_keys[6], 71), 0)
    kv_pool = draw_kv_pool(jax.random.fold_in(arg_keys[6], 71), 0)
    window_table = draw_window_table(jax.random.fold_in(arg_keys[6], 71), 0)
    append_table = draw_append_table(jax.random.fold_in(arg_keys[6], 71), 0)
    cache_lengths = draw_cache_lengths(jax.random.fold_in(arg_keys[6], 71), 0)
    return dict(queries=queries, new_kv=new_kv, kv_pool=kv_pool, window_table=window_table, append_table=append_table, cache_lengths=cache_lengths)


def attend_block(query_rows, keys_use, index_use, live_use, block_start):
    block_len = query_rows.shape[0]
    scores = jnp.einsum("thd,kd->thk", query_rows.astype(jnp.float32), keys_use[:, :DH].astype(jnp.float32)) * (DH ** -0.5)
    positions = block_start + jnp.arange(block_len).astype(jnp.int32)
    allowed = (index_use[None, :] > positions[:, None]) & (index_use[None, :] <= positions[:, None] + W) & live_use[None, :]
    scores = jnp.where(allowed[:, None, :], scores, -jnp.inf)
    row_max = jnp.max(scores, axis=2, keepdims=True)
    raw_weights = jnp.exp(scores - row_max)
    row_total = jnp.sum(raw_weights, axis=2, keepdims=True)
    weights = raw_weights.astype(jnp.bfloat16)
    weighted = jnp.einsum("thk,kd->thd", weights.astype(jnp.float32), keys_use[:, DH:].astype(jnp.float32))
    return (weighted / row_total).astype(jnp.bfloat16)


def reference(queries, new_kv, kv_pool, window_table, append_table, cache_lengths):
    block_len = min(128, CH)
    block_count = CH // block_len

    def one_request(inputs):
        query_rows, fresh_keys, page_ids, own_length = inputs
        cached = kv_pool[page_ids.astype(jnp.int32)].reshape(W, 2 * DH)
        keys_all = jnp.concatenate([cached, fresh_keys], axis=0)
        key_index = jnp.arange(W + CH).astype(jnp.int32)
        filled = jnp.minimum(own_length // PAGE, WP)
        live_keys = (key_index >= W) | (key_index // PAGE >= WP - filled)
        blocks_in = query_rows.reshape(block_count, block_len, H, DH)
        offsets = (jnp.arange(block_count) * block_len).astype(jnp.int32)

        def one_block(block_pair):
            qblock, block_start = block_pair
            keys_use = lax.dynamic_slice_in_dim(keys_all, block_start, W + block_len, 0)
            index_use = block_start + jnp.arange(W + block_len).astype(jnp.int32)
            live_use = lax.dynamic_slice_in_dim(live_keys, block_start, W + block_len, 0)
            return attend_block(qblock, keys_use, index_use, live_use, block_start)

        return lax.map(one_block, (blocks_in, offsets)).reshape(CH, H * DH)

    attn_out = lax.map(one_request, (queries, new_kv, window_table, cache_lengths))
    new_pool = kv_pool.at[append_table.reshape(-1).astype(jnp.int32)].set(new_kv.reshape(REQS * NPN, PAGE, 2 * DH))
    return attn_out, new_pool
```

```python
import jax
import jax.numpy as jnp
from jax import lax
from jax.sharding import PartitionSpec as P


def earlier_same(owners):
    slot_count = owners.shape[1]
    same_owner = owners[:, :, None] == owners[:, None, :]
    before = jnp.arange(slot_count)[None, :] < jnp.arange(slot_count)[:, None]
    return jnp.sum(same_owner & before[None, :, :], axis=2)


def pick_rows(wanted, values):
    return jnp.sum(jnp.where(wanted, values[:, None, :], 0), axis=2)


def attend(qblock, keys_use, index_use, live_use, block_start, head_count, head_size, window_len):
    block_len = qblock.shape[0]
    query_rows = qblock.reshape(block_len, head_count, head_size)
    scores = jnp.einsum(
        "thd,kd->thk", query_rows, keys_use[:, :head_size], preferred_element_type=jnp.float32
    ) * head_size ** (-0.5)
    positions = block_start + jnp.arange(block_len)
    allowed = (
        (index_use[None, :] > positions[:, None])
        & (index_use[None, :] <= positions[:, None] + window_len)
        & live_use[None, :]
    )
    scores = jnp.where(allowed[:, None, :], scores, -jnp.inf)
    row_max = jnp.max(scores, axis=2, keepdims=True)
    raw_weights = jnp.exp(scores - row_max)
    row_total = jnp.sum(raw_weights, axis=2, keepdims=True)
    weights = raw_weights.astype(jnp.bfloat16)
    weighted = jnp.einsum(
        "thk,kd->thd", weights, keys_use[:, head_size:], preferred_element_type=jnp.float32
    )
    return (weighted / row_total).astype(jnp.bfloat16).reshape(block_len, head_count * head_size)


def regroup(pieces):
    groups, pages, piece_rows, width = pieces.shape
    return pieces.transpose(1, 0, 2, 3).reshape(pages, groups * piece_rows, width)


def shards(queries, new_kv, kv_pool, window_table, append_table, cache_lengths):
    blocks = lax.axis_size("blk")
    groups = lax.axis_size("group")
    my_block = lax.axis_index("blk")
    piece_index = lax.axis_index("group")
    tok_rows = queries.shape[1]
    per_owner = kv_pool.shape[0]
    page_rows = kv_pool.shape[1]
    key_width = kv_pool.shape[2]
    head_size = key_width // 2
    head_count = queries.shape[2] // head_size
    win_pages = window_table.shape[1]
    new_pages = append_table.shape[1]
    win_rows = win_pages * page_rows
    cap_win = (win_pages + blocks - 1) // blocks
    cap_new = (new_pages + blocks - 1) // blocks
    piece_rows = page_rows // groups
    piece_start = piece_index * piece_rows
    fresh_keys = lax.all_gather(new_kv, "group", axis=1, tiled=True)[0]
    append_rows = fresh_keys.shape[0]

    win_owner = window_table // per_owner
    win_rank = earlier_same(win_owner)
    win_wanted = (win_owner == my_block)[:, None, :] & (
        win_rank[:, None, :] == jnp.arange(cap_win)[None, :, None]
    )
    send_ids = pick_rows(win_wanted, window_table % per_owner)
    own_owner = lax.dynamic_index_in_dim(win_owner, my_block, 0, keepdims=False)
    own_rank = lax.dynamic_index_in_dim(win_rank, my_block, 0, keepdims=False)
    arrival = own_owner * cap_win + own_rank
    pool_piece = lax.dynamic_slice_in_dim(kv_pool, piece_start, piece_rows, axis=1)
    outgoing = pool_piece[send_ids.reshape(-1)]
    received = lax.all_to_all(outgoing, "blk", split_axis=0, concat_axis=0, tiled=True)
    cached_piece = received[arrival]
    cached = regroup(lax.all_gather(cached_piece, "group", axis=0, tiled=False))

    new_owner = append_table // per_owner
    new_rank = earlier_same(new_owner)
    mine_owner = lax.dynamic_index_in_dim(new_owner, my_block, 0, keepdims=False)
    mine_rank = lax.dynamic_index_in_dim(new_rank, my_block, 0, keepdims=False)
    dest_wanted = (mine_owner[None, None, :] == jnp.arange(blocks)[:, None, None]) & (
        mine_rank[None, None, :] == jnp.arange(cap_new)[None, :, None]
    )
    page_pick = jnp.sum(jnp.where(dest_wanted, jnp.arange(new_pages)[None, None, :], 0), axis=2)
    fresh_pages = fresh_keys.reshape(new_pages, page_rows, key_width)
    fresh_piece = lax.dynamic_slice_in_dim(fresh_pages, piece_start, piece_rows, axis=1)
    parcels = fresh_piece[page_pick.reshape(-1)]
    arrived = lax.all_to_all(parcels, "blk", split_axis=0, concat_axis=0, tiled=True)
    land_here = new_owner == my_block
    land_source = jnp.argmax(land_here, axis=0)
    land_slot = land_source * cap_new + jnp.take_along_axis(new_rank, land_source[None, :], axis=0)[0]
    land_ids = jnp.take_along_axis(append_table % per_owner, land_source[None, :], axis=0)[0]
    land_live = jnp.any(land_here, axis=0)
    landed = regroup(lax.all_gather(arrived[land_slot], "group", axis=0, tiled=False))
    targets = jnp.where(land_live, land_ids, per_owner)
    new_pool = kv_pool.at[targets].set(landed, mode="drop")

    keys_all = jnp.concatenate([cached.reshape(win_rows, key_width), fresh_keys], axis=0)
    own_length = lax.dynamic_index_in_dim(cache_lengths, my_block, 0, keepdims=False)
    filled = jnp.minimum(own_length // page_rows, win_pages)
    key_index = jnp.arange(win_rows + append_rows)
    live_keys = (key_index >= win_rows) | (key_index // page_rows >= win_pages - filled)
    block_len = min(128, tok_rows)
    block_count = tok_rows // block_len
    query_blocks = queries[0].reshape(block_count, block_len, queries.shape[2])
    first_row = piece_index * tok_rows
    offsets = jnp.arange(block_count) * block_len
    span = win_rows + block_len

    def one_block(inputs):
        qblock, offset = inputs
        block_start = first_row + offset
        keys_use = lax.dynamic_slice_in_dim(keys_all, block_start, span, 0)
        index_use = block_start + jnp.arange(span)
        live_use = lax.dynamic_slice_in_dim(live_keys, block_start, span, 0)
        return attend(
            qblock, keys_use, index_use, live_use, block_start, head_count, head_size, win_rows
        )

    attended = lax.map(one_block, (query_blocks, offsets))
    attn_out = attended.reshape(1, tok_rows, queries.shape[2])
    return (attn_out, new_pool)


def solution(mesh):
    in_specs = (
        P("blk", "group", None),
        P("blk", "group", None),
        P("blk", None, None),
        P(),
        P(),
        P(),
    )
    out_specs = (P("blk", "group", None), P("blk", None, None))
    return jax.shard_map(shards, mesh=mesh, in_specs=in_specs, out_specs=out_specs, check_vma=False)
```

```python
import jax
import jax.numpy as jnp
from jax import lax
from jax.sharding import Mesh, PartitionSpec as P


def earlier_same(owners):
    slot_count = owners.shape[1]
    same_owner = owners[:, :, None] == owners[:, None, :]
    before = jnp.arange(slot_count)[None, :] < jnp.arange(slot_count)[:, None]
    return jnp.sum(same_owner & before[None, :, :], axis=2)


def pick_rows(wanted, values):
    return jnp.sum(jnp.where(wanted, values[:, None, :], 0), axis=2)


def attend(qblock, keys_use, index_use, live_use, block_start, head_count, head_size, window_len):
    block_len = qblock.shape[0]
    query_rows = qblock.reshape(block_len, head_count, head_size)
    scores = jnp.einsum(
        "thd,kd->thk", query_rows, keys_use[:, :head_size], preferred_element_type=jnp.float32
    ) * head_size ** (-0.5)
    positions = block_start + jnp.arange(block_len)
    allowed = (
        (index_use[None, :] > positions[:, None])
        & (index_use[None, :] <= positions[:, None] + window_len)
        & live_use[None, :]
    )
    scores = jnp.where(allowed[:, None, :], scores, -jnp.inf)
    row_max = jnp.max(scores, axis=2, keepdims=True)
    raw_weights = jnp.exp(scores - row_max)
    row_total = jnp.sum(raw_weights, axis=2, keepdims=True)
    weights = raw_weights.astype(jnp.bfloat16)
    weighted = jnp.einsum(
        "thk,kd->thd", weights, keys_use[:, head_size:], preferred_element_type=jnp.float32
    )
    return (weighted / row_total).astype(jnp.bfloat16).reshape(block_len, head_count * head_size)


def regroup(pieces):
    groups, pages, piece_rows, width = pieces.shape
    return pieces.transpose(1, 0, 2, 3).reshape(pages, groups * piece_rows, width)


def spread(pieces, axis_name, count):
    copies = jnp.broadcast_to(pieces[None], (count,) + pieces.shape)
    return lax.all_to_all(copies, axis_name, 0, 0, tiled=False)


def group_gather(pieces, cores):
    chips = lax.axis_size("gx")
    over_chips = spread(pieces, "gx", chips)
    both = spread(over_chips, "gc", cores)
    return both.transpose(1, 0, *range(2, both.ndim)).reshape((chips * cores,) + pieces.shape)


def shards(queries, new_kv, kv_pool, window_table, append_table, cache_lengths):
    blocks = lax.axis_size("blk")
    cores = lax.axis_size("gc")
    groups = lax.axis_size("gx") * cores
    my_block = lax.axis_index("blk")
    piece_index = lax.axis_index("gx") * cores + lax.axis_index("gc")
    tok_rows = queries.shape[1]
    per_owner = kv_pool.shape[0]
    page_rows = kv_pool.shape[1]
    key_width = kv_pool.shape[2]
    head_size = key_width // 2
    head_count = queries.shape[2] // head_size
    win_pages = window_table.shape[1]
    new_pages = append_table.shape[1]
    win_rows = win_pages * page_rows
    cap_win = (win_pages + blocks - 1) // blocks
    cap_new = (new_pages + blocks - 1) // blocks
    piece_rows = page_rows // groups
    piece_start = piece_index * piece_rows
    fresh_keys = lax.all_gather(new_kv, ("gx", "gc"), axis=1, tiled=True)[0]
    append_rows = fresh_keys.shape[0]

    win_owner = window_table // per_owner
    win_rank = earlier_same(win_owner)
    win_wanted = (win_owner == my_block)[:, None, :] & (
        win_rank[:, None, :] == jnp.arange(cap_win)[None, :, None]
    )
    send_ids = pick_rows(win_wanted, window_table % per_owner)
    own_owner = lax.dynamic_index_in_dim(win_owner, my_block, 0, keepdims=False)
    own_rank = lax.dynamic_index_in_dim(win_rank, my_block, 0, keepdims=False)
    arrival = own_owner * cap_win + own_rank
    pool_piece = lax.dynamic_slice_in_dim(kv_pool, piece_start, piece_rows, axis=1)
    outgoing = pool_piece[send_ids.reshape(-1)]
    received = lax.all_to_all(outgoing, "blk", split_axis=0, concat_axis=0, tiled=True)
    cached_piece = received[arrival]
    cached = regroup(lax.all_gather(cached_piece, ("gx", "gc"), axis=0, tiled=False))

    new_owner = append_table // per_owner
    new_rank = earlier_same(new_owner)
    mine_owner = lax.dynamic_index_in_dim(new_owner, my_block, 0, keepdims=False)
    mine_rank = lax.dynamic_index_in_dim(new_rank, my_block, 0, keepdims=False)
    dest_wanted = (mine_owner[None, None, :] == jnp.arange(blocks)[:, None, None]) & (
        mine_rank[None, None, :] == jnp.arange(cap_new)[None, :, None]
    )
    page_pick = jnp.sum(jnp.where(dest_wanted, jnp.arange(new_pages)[None, None, :], 0), axis=2)
    own_pages = new_kv[0].reshape(-1, groups, piece_rows, key_width).transpose(1, 0, 2, 3)
    fresh_piece = lax.all_to_all(own_pages, ("gx", "gc"), 0, 0, tiled=True).reshape(new_pages, piece_rows, key_width)
    parcels = fresh_piece[page_pick.reshape(-1)]
    arrived = lax.all_to_all(parcels, "blk", split_axis=0, concat_axis=0, tiled=True)
    land_here = new_owner == my_block
    land_source = jnp.argmax(land_here, axis=0)
    land_slot = land_source * cap_new + jnp.take_along_axis(new_rank, land_source[None, :], axis=0)[0]
    land_ids = jnp.take_along_axis(append_table % per_owner, land_source[None, :], axis=0)[0]
    land_live = jnp.any(land_here, axis=0)
    landed = regroup(group_gather(arrived[land_slot], cores))
    targets = jnp.where(land_live, land_ids, per_owner)
    new_pool = kv_pool.at[targets].set(landed, mode="drop")

    keys_all = jnp.concatenate([cached.reshape(win_rows, key_width), fresh_keys], axis=0)
    own_length = lax.dynamic_index_in_dim(cache_lengths, my_block, 0, keepdims=False)
    filled = jnp.minimum(own_length // page_rows, win_pages)
    key_index = jnp.arange(win_rows + append_rows)
    live_keys = (key_index >= win_rows) | (key_index // page_rows >= win_pages - filled)
    block_len = min(128, tok_rows)
    block_count = tok_rows // block_len
    query_blocks = queries[0].reshape(block_count, block_len, queries.shape[2])
    first_row = piece_index * tok_rows
    offsets = jnp.arange(block_count) * block_len
    span = win_rows + block_len

    def one_block(inputs):
        qblock, offset = inputs
        block_start = first_row + offset
        keys_use = lax.dynamic_slice_in_dim(keys_all, block_start, span, 0)
        index_use = block_start + jnp.arange(span)
        live_use = lax.dynamic_slice_in_dim(live_keys, block_start, span, 0)
        return attend(
            qblock, keys_use, index_use, live_use, block_start, head_count, head_size, win_rows
        )

    attended = lax.map(one_block, (query_blocks, offsets))
    attn_out = attended.reshape(1, tok_rows, queries.shape[2])
    return (attn_out, new_pool)


def solution(mesh):
    chip_count = mesh.shape["group"] // 2
    split = Mesh(mesh.devices.reshape(mesh.shape["blk"], chip_count, 2), ("blk", "gx", "gc"))
    tokens = ("gx", "gc")
    in_specs = (
        P("blk", tokens, None),
        P("blk", tokens, None),
        P("blk", None, None),
        P(),
        P(),
        P(),
    )
    out_specs = (P("blk", tokens, None), P("blk", None, None))
    return jax.shard_map(shards, mesh=split, in_specs=in_specs, out_specs=out_specs, check_vma=False)
```

```python
import functools

import jax
import jax.numpy as jnp
from jax import lax
from jax.experimental import pallas as pl
from jax.experimental.pallas import tpu as pltpu
from jax.sharding import PartitionSpec as P


def earlier_same(owners):
    slot_count = owners.shape[1]
    same_owner = owners[:, :, None] == owners[:, None, :]
    before = jnp.arange(slot_count)[None, :] < jnp.arange(slot_count)[:, None]
    return jnp.sum(same_owner & before[None, :, :], axis=2)


def pick_rows(wanted, values):
    return jnp.sum(jnp.where(wanted, values[:, None, :], 0), axis=2)


def attend(qblock, keys_use, index_use, live_use, block_start, head_count, head_size, window_len):
    block_len = qblock.shape[0]
    query_rows = qblock.reshape(block_len, head_count, head_size)
    scores = jnp.einsum(
        "thd,kd->thk", query_rows, keys_use[:, :head_size], preferred_element_type=jnp.float32
    ) * head_size ** (-0.5)
    positions = block_start + jnp.arange(block_len)
    allowed = (
        (index_use[None, :] > positions[:, None])
        & (index_use[None, :] <= positions[:, None] + window_len)
        & live_use[None, :]
    )
    scores = jnp.where(allowed[:, None, :], scores, -jnp.inf)
    row_max = jnp.max(scores, axis=2, keepdims=True)
    raw_weights = jnp.exp(scores - row_max)
    row_total = jnp.sum(raw_weights, axis=2, keepdims=True)
    weights = raw_weights.astype(jnp.bfloat16)
    weighted = jnp.einsum(
        "thk,kd->thd", weights, keys_use[:, head_size:], preferred_element_type=jnp.float32
    )
    return (weighted / row_total).astype(jnp.bfloat16).reshape(block_len, head_count * head_size)


def regroup(pieces):
    groups, pages, piece_rows, width = pieces.shape
    return pieces.transpose(1, 0, 2, 3).reshape(pages, groups * piece_rows, width)


def window_kernel(meta, q_ref, cached_hbm, fresh_hbm, out_ref, keys, bias, sems, *, chunk, chunks,
                  split, head_count, head_size, window_len):
    first = meta[0]
    live_from = meta[1]

    def chunk_copy(c, begin):
        j = first + c

        @pl.when(j < split)
        def _():
            cp = pltpu.make_async_copy(
                cached_hbm.at[pl.ds(j * chunk, chunk)], keys.at[pl.ds(c * chunk, chunk)], sems.at[c]
            )
            cp.start() if begin else cp.wait()

        @pl.when(j >= split)
        def _():
            cp = pltpu.make_async_copy(
                fresh_hbm.at[pl.ds((j - split) * chunk, chunk)], keys.at[pl.ds(c * chunk, chunk)], sems.at[c]
            )
            cp.start() if begin else cp.wait()

    for c in range(chunks):
        chunk_copy(c, True)
    rows = lax.broadcasted_iota(jnp.int32, bias.shape, 0)
    cols = lax.broadcasted_iota(jnp.int32, bias.shape, 1)
    allowed = (cols > rows) & (cols <= rows + window_len) & (cols >= live_from)
    bias[...] = jnp.where(allowed, 0.0, -jnp.inf).astype(jnp.float32)
    for c in range(chunks):
        chunk_copy(c, False)
    scale = head_size ** (-0.5)

    def one_head(h, carry):
        lanes = pl.ds(pl.multiple_of(h * head_size, head_size), head_size)
        scores = lax.dot_general(
            q_ref[:, lanes], keys[:, :head_size], (((1,), (1,)), ((), ())),
            preferred_element_type=jnp.float32,
        )
        scores = scores * scale + bias[...]
        row_max = jnp.max(scores, axis=1, keepdims=True)
        raw_weights = jnp.exp(scores - row_max)
        row_total = jnp.sum(raw_weights, axis=1, keepdims=True)
        weighted = jnp.dot(
            raw_weights.astype(jnp.bfloat16), keys[:, head_size:], preferred_element_type=jnp.float32
        )
        out_ref[:, lanes] = (weighted / row_total).astype(out_ref.dtype)
        return carry

    lax.fori_loop(0, head_count, one_head, 0)


def window_attention(query_rows, cached, fresh, first_chunk, live_from, head_count, head_size, window_len):
    tok_rows, width = query_rows.shape
    chunk = tok_rows
    span = window_len + tok_rows
    chunks = span // chunk
    split = cached.shape[0] // chunk
    key_width = cached.shape[1]
    body = functools.partial(
        window_kernel, chunk=chunk, chunks=chunks, split=split, head_count=head_count,
        head_size=head_size, window_len=window_len,
    )
    meta = jnp.stack([first_chunk, live_from]).astype(jnp.int32)
    return pl.pallas_call(
        body,
        out_shape=jax.ShapeDtypeStruct((tok_rows, width), query_rows.dtype),
        grid_spec=pltpu.PrefetchScalarGridSpec(
            num_scalar_prefetch=1,
            grid=(1,),
            in_specs=[
                pl.BlockSpec((tok_rows, width), lambda i, m: (0, 0)),
                pl.BlockSpec(memory_space=pl.ANY),
                pl.BlockSpec(memory_space=pl.ANY),
            ],
            out_specs=pl.BlockSpec((tok_rows, width), lambda i, m: (0, 0)),
            scratch_shapes=[
                pltpu.VMEM((span, key_width), cached.dtype),
                pltpu.VMEM((tok_rows, span), jnp.float32),
                pltpu.SemaphoreType.DMA((chunks,)),
            ],
        ),
        compiler_params=pltpu.CompilerParams(vmem_limit_bytes=48 * 1024 * 1024),
    )(meta, query_rows, cached, fresh)


def shards(queries, new_kv, kv_pool, window_table, append_table, cache_lengths):
    blocks = lax.axis_size("blk")
    groups = lax.axis_size("group")
    my_block = lax.axis_index("blk")
    piece_index = lax.axis_index("group")
    tok_rows = queries.shape[1]
    per_owner = kv_pool.shape[0]
    page_rows = kv_pool.shape[1]
    key_width = kv_pool.shape[2]
    head_size = key_width // 2
    head_count = queries.shape[2] // head_size
    win_pages = window_table.shape[1]
    new_pages = append_table.shape[1]
    win_rows = win_pages * page_rows
    cap_win = (win_pages + blocks - 1) // blocks
    cap_new = (new_pages + blocks - 1) // blocks
    piece_rows = page_rows // groups
    piece_start = piece_index * piece_rows
    fresh_keys = lax.all_gather(new_kv, "group", axis=1, tiled=True)[0]
    append_rows = fresh_keys.shape[0]

    win_owner = window_table // per_owner
    win_rank = earlier_same(win_owner)
    win_wanted = (win_owner == my_block)[:, None, :] & (
        win_rank[:, None, :] == jnp.arange(cap_win)[None, :, None]
    )
    send_ids = pick_rows(win_wanted, window_table % per_owner)
    own_owner = lax.dynamic_index_in_dim(win_owner, my_block, 0, keepdims=False)
    own_rank = lax.dynamic_index_in_dim(win_rank, my_block, 0, keepdims=False)
    arrival = own_owner * cap_win + own_rank
    pool_piece = lax.dynamic_slice_in_dim(kv_pool, piece_start, piece_rows, axis=1)
    outgoing = pool_piece[send_ids.reshape(-1)]
    received = lax.all_to_all(outgoing, "blk", split_axis=0, concat_axis=0, tiled=True)
    cached_piece = received[arrival]
    cached = regroup(lax.all_gather(cached_piece, "group", axis=0, tiled=False))

    new_owner = append_table // per_owner
    new_rank = earlier_same(new_owner)
    mine_owner = lax.dynamic_index_in_dim(new_owner, my_block, 0, keepdims=False)
    mine_rank = lax.dynamic_index_in_dim(new_rank, my_block, 0, keepdims=False)
    dest_wanted = (mine_owner[None, None, :] == jnp.arange(blocks)[:, None, None]) & (
        mine_rank[None, None, :] == jnp.arange(cap_new)[None, :, None]
    )
    page_pick = jnp.sum(jnp.where(dest_wanted, jnp.arange(new_pages)[None, None, :], 0), axis=2)
    fresh_pages = fresh_keys.reshape(new_pages, page_rows, key_width)
    fresh_piece = lax.dynamic_slice_in_dim(fresh_pages, piece_start, piece_rows, axis=1)
    parcels = fresh_piece[page_pick.reshape(-1)]
    arrived = lax.all_to_all(parcels, "blk", split_axis=0, concat_axis=0, tiled=True)
    land_here = new_owner == my_block
    land_source = jnp.argmax(land_here, axis=0)
    land_slot = land_source * cap_new + jnp.take_along_axis(new_rank, land_source[None, :], axis=0)[0]
    land_ids = jnp.take_along_axis(append_table % per_owner, land_source[None, :], axis=0)[0]
    land_live = jnp.any(land_here, axis=0)
    landed = regroup(lax.all_gather(arrived[land_slot], "group", axis=0, tiled=False))
    targets = jnp.where(land_live, land_ids, per_owner)
    new_pool = kv_pool.at[targets].set(landed, mode="drop")

    own_length = lax.dynamic_index_in_dim(cache_lengths, my_block, 0, keepdims=False)
    filled = jnp.minimum(own_length // page_rows, win_pages)
    first_row = piece_index * tok_rows
    live_from = (win_pages - filled) * page_rows - first_row
    attended = window_attention(
        queries[0], cached.reshape(win_rows, key_width), fresh_keys, piece_index, live_from,
        head_count, head_size, win_rows,
    )
    attn_out = attended.reshape(1, tok_rows, queries.shape[2])
    return (attn_out, new_pool)


def solution(mesh):
    in_specs = (
        P("blk", "group", None),
        P("blk", "group", None),
        P("blk", None, None),
        P(),
        P(),
        P(),
    )
    out_specs = (P("blk", "group", None), P("blk", None, None))
    return jax.shard_map(shards, mesh=mesh, in_specs=in_specs, out_specs=out_specs, check_vma=False)
```

```python
import functools

import jax
import jax.numpy as jnp
from jax import lax
from jax.experimental import pallas as pl
from jax.experimental.pallas import tpu as pltpu
from jax.sharding import PartitionSpec as P


def earlier_same(owners):
    slot_count = owners.shape[1]
    same_owner = owners[:, :, None] == owners[:, None, :]
    before = jnp.arange(slot_count)[None, :] < jnp.arange(slot_count)[:, None]
    return jnp.sum(same_owner & before[None, :, :], axis=2)


def pick_rows(wanted, values):
    return jnp.sum(jnp.where(wanted, values[:, None, :], 0), axis=2)


def attend(qblock, keys_use, index_use, live_use, block_start, head_count, head_size, window_len):
    block_len = qblock.shape[0]
    query_rows = qblock.reshape(block_len, head_count, head_size)
    scores = jnp.einsum(
        "thd,kd->thk", query_rows, keys_use[:, :head_size], preferred_element_type=jnp.float32
    ) * head_size ** (-0.5)
    positions = block_start + jnp.arange(block_len)
    allowed = (
        (index_use[None, :] > positions[:, None])
        & (index_use[None, :] <= positions[:, None] + window_len)
        & live_use[None, :]
    )
    scores = jnp.where(allowed[:, None, :], scores, -jnp.inf)
    row_max = jnp.max(scores, axis=2, keepdims=True)
    raw_weights = jnp.exp(scores - row_max)
    row_total = jnp.sum(raw_weights, axis=2, keepdims=True)
    weights = raw_weights.astype(jnp.bfloat16)
    weighted = jnp.einsum(
        "thk,kd->thd", weights, keys_use[:, head_size:], preferred_element_type=jnp.float32
    )
    return (weighted / row_total).astype(jnp.bfloat16).reshape(block_len, head_count * head_size)


def regroup(pieces):
    groups, pages, piece_rows, width = pieces.shape
    return pieces.transpose(1, 0, 2, 3).reshape(pages, groups * piece_rows, width)


def window_kernel(meta, q_ref, cached_hbm, fresh_hbm, out_ref, keys, bias, sems, *, chunk, chunks,
                  split, head_count, head_size, window_len):
    groups, _, piece_rows, _ = cached_hbm.shape
    page_rows = groups * piece_rows
    pages_per_chunk = chunk // page_rows
    first = meta[0]
    live_from = meta[1]

    def chunk_copy(c, begin):
        j = first + c

        @pl.when(j < split)
        def _():
            if begin:
                for p in range(pages_per_chunk):
                    for grp in range(groups):
                        pltpu.make_async_copy(
                            cached_hbm.at[grp, j * pages_per_chunk + p],
                            keys.at[pl.ds(c * chunk + p * page_rows + grp * piece_rows, piece_rows)],
                            sems.at[c],
                        ).start()
            else:
                pltpu.make_async_copy(
                    fresh_hbm.at[pl.ds(0, chunk)], keys.at[pl.ds(c * chunk, chunk)], sems.at[c]
                ).wait()

        @pl.when(j >= split)
        def _():
            cp = pltpu.make_async_copy(
                fresh_hbm.at[pl.ds((j - split) * chunk, chunk)], keys.at[pl.ds(c * chunk, chunk)], sems.at[c]
            )
            cp.start() if begin else cp.wait()

    for c in range(chunks):
        chunk_copy(c, True)
    rows = lax.broadcasted_iota(jnp.int32, bias.shape, 0)
    cols = lax.broadcasted_iota(jnp.int32, bias.shape, 1)
    allowed = (cols > rows) & (cols <= rows + window_len) & (cols >= live_from)
    bias[...] = jnp.where(allowed, 0.0, -jnp.inf).astype(jnp.float32)
    for c in range(chunks):
        chunk_copy(c, False)
    scale = head_size ** (-0.5)

    def one_head(h, carry):
        lanes = pl.ds(pl.multiple_of(h * head_size, head_size), head_size)
        scores = lax.dot_general(
            q_ref[:, lanes], keys[:, :head_size], (((1,), (1,)), ((), ())),
            preferred_element_type=jnp.float32,
        )
        scores = scores * scale + bias[...]
        row_max = jnp.max(scores, axis=1, keepdims=True)
        raw_weights = jnp.exp(scores - row_max)
        row_total = jnp.sum(raw_weights, axis=1, keepdims=True)
        weighted = jnp.dot(
            raw_weights.astype(jnp.bfloat16), keys[:, head_size:], preferred_element_type=jnp.float32
        )
        out_ref[:, lanes] = (weighted / row_total).astype(out_ref.dtype)
        return carry

    lax.fori_loop(0, head_count, one_head, 0)


def window_attention(query_rows, cached, fresh, first_chunk, live_from, head_count, head_size, window_len):
    tok_rows, width = query_rows.shape
    chunk = tok_rows
    span = window_len + tok_rows
    chunks = span // chunk
    groups, pages, piece_rows, key_width = cached.shape
    split = pages * groups * piece_rows // chunk
    body = functools.partial(
        window_kernel, chunk=chunk, chunks=chunks, split=split, head_count=head_count,
        head_size=head_size, window_len=window_len,
    )
    meta = jnp.stack([first_chunk, live_from]).astype(jnp.int32)
    return pl.pallas_call(
        body,
        out_shape=jax.ShapeDtypeStruct((tok_rows, width), query_rows.dtype),
        grid_spec=pltpu.PrefetchScalarGridSpec(
            num_scalar_prefetch=1,
            grid=(1,),
            in_specs=[
                pl.BlockSpec((tok_rows, width), lambda i, m: (0, 0)),
                pl.BlockSpec(memory_space=pl.ANY),
                pl.BlockSpec(memory_space=pl.ANY),
            ],
            out_specs=pl.BlockSpec((tok_rows, width), lambda i, m: (0, 0)),
            scratch_shapes=[
                pltpu.VMEM((span, key_width), cached.dtype),
                pltpu.VMEM((tok_rows, span), jnp.float32),
                pltpu.SemaphoreType.DMA((chunks,)),
            ],
        ),
        compiler_params=pltpu.CompilerParams(vmem_limit_bytes=48 * 1024 * 1024),
    )(meta, query_rows, cached, fresh)


def pool_kernel(source, pool_hbm, landed_hbm, out_hbm, sems):
    groups, _, piece_rows, _ = landed_hbm.shape
    for page in range(pool_hbm.shape[0]):
        picked = source[page]

        @pl.when(picked < 0)
        def _():
            pltpu.make_async_copy(pool_hbm.at[page], out_hbm.at[page], sems.at[page]).start()

        @pl.when(picked >= 0)
        def _():
            for grp in range(groups):
                pltpu.make_async_copy(
                    landed_hbm.at[grp, picked],
                    out_hbm.at[page, pl.ds(grp * piece_rows, piece_rows)],
                    sems.at[page],
                ).start()

    for page in range(pool_hbm.shape[0]):
        pltpu.make_async_copy(pool_hbm.at[page], out_hbm.at[page], sems.at[page]).wait()


def write_pool(kv_pool, landed_pieces, targets):
    pages = kv_pool.shape[0]
    source = jnp.full((pages,), -1, jnp.int32).at[targets].set(
        jnp.arange(targets.shape[0], dtype=jnp.int32), mode="drop"
    )
    return pl.pallas_call(
        pool_kernel,
        out_shape=jax.ShapeDtypeStruct(kv_pool.shape, kv_pool.dtype),
        grid_spec=pltpu.PrefetchScalarGridSpec(
            num_scalar_prefetch=1,
            grid=(1,),
            in_specs=[pl.BlockSpec(memory_space=pl.ANY), pl.BlockSpec(memory_space=pl.ANY)],
            out_specs=pl.BlockSpec(memory_space=pl.ANY),
            scratch_shapes=[pltpu.SemaphoreType.DMA((pages,))],
        ),
    )(source, kv_pool, landed_pieces)


def shards(queries, new_kv, kv_pool, window_table, append_table, cache_lengths):
    blocks = lax.axis_size("blk")
    groups = lax.axis_size("group")
    my_block = lax.axis_index("blk")
    piece_index = lax.axis_index("group")
    tok_rows = queries.shape[1]
    per_owner = kv_pool.shape[0]
    page_rows = kv_pool.shape[1]
    key_width = kv_pool.shape[2]
    head_size = key_width // 2
    head_count = queries.shape[2] // head_size
    win_pages = window_table.shape[1]
    new_pages = append_table.shape[1]
    win_rows = win_pages * page_rows
    cap_win = (win_pages + blocks - 1) // blocks
    cap_new = (new_pages + blocks - 1) // blocks
    piece_rows = page_rows // groups
    piece_start = piece_index * piece_rows
    fresh_keys = lax.all_gather(new_kv, "group", axis=1, tiled=True)[0]
    append_rows = fresh_keys.shape[0]

    win_owner = window_table // per_owner
    win_rank = earlier_same(win_owner)
    win_wanted = (win_owner == my_block)[:, None, :] & (
        win_rank[:, None, :] == jnp.arange(cap_win)[None, :, None]
    )
    send_ids = pick_rows(win_wanted, window_table % per_owner)
    own_owner = lax.dynamic_index_in_dim(win_owner, my_block, 0, keepdims=False)
    own_rank = lax.dynamic_index_in_dim(win_rank, my_block, 0, keepdims=False)
    arrival = own_owner * cap_win + own_rank
    pool_piece = lax.dynamic_slice_in_dim(kv_pool, piece_start, piece_rows, axis=1)
    outgoing = pool_piece[send_ids.reshape(-1)]
    received = lax.all_to_all(outgoing, "blk", split_axis=0, concat_axis=0, tiled=True)
    cached_piece = received[arrival]
    cached_pieces = lax.all_gather(cached_piece, "group", axis=0, tiled=False)

    new_owner = append_table // per_owner
    new_rank = earlier_same(new_owner)
    mine_owner = lax.dynamic_index_in_dim(new_owner, my_block, 0, keepdims=False)
    mine_rank = lax.dynamic_index_in_dim(new_rank, my_block, 0, keepdims=False)
    dest_wanted = (mine_owner[None, None, :] == jnp.arange(blocks)[:, None, None]) & (
        mine_rank[None, None, :] == jnp.arange(cap_new)[None, :, None]
    )
    page_pick = jnp.sum(jnp.where(dest_wanted, jnp.arange(new_pages)[None, None, :], 0), axis=2)
    fresh_pages = fresh_keys.reshape(new_pages, page_rows, key_width)
    fresh_piece = lax.dynamic_slice_in_dim(fresh_pages, piece_start, piece_rows, axis=1)
    parcels = fresh_piece[page_pick.reshape(-1)]
    arrived = lax.all_to_all(parcels, "blk", split_axis=0, concat_axis=0, tiled=True)
    land_here = new_owner == my_block
    land_source = jnp.argmax(land_here, axis=0)
    land_slot = land_source * cap_new + jnp.take_along_axis(new_rank, land_source[None, :], axis=0)[0]
    land_ids = jnp.take_along_axis(append_table % per_owner, land_source[None, :], axis=0)[0]
    land_live = jnp.any(land_here, axis=0)
    landed = lax.all_gather(arrived[land_slot], "group", axis=0, tiled=False)
    targets = jnp.where(land_live, land_ids, per_owner)
    new_pool = write_pool(kv_pool, landed, targets)

    own_length = lax.dynamic_index_in_dim(cache_lengths, my_block, 0, keepdims=False)
    filled = jnp.minimum(own_length // page_rows, win_pages)
    first_row = piece_index * tok_rows
    live_from = (win_pages - filled) * page_rows - first_row
    attended = window_attention(
        queries[0], cached_pieces, fresh_keys, piece_index, live_from,
        head_count, head_size, win_rows,
    )
    attn_out = attended.reshape(1, tok_rows, queries.shape[2])
    return (attn_out, new_pool)


def solution(mesh):
    in_specs = (
        P("blk", "group", None),
        P("blk", "group", None),
        P("blk", None, None),
        P(),
        P(),
        P(),
    )
    out_specs = (P("blk", "group", None), P("blk", None, None))
    return jax.shard_map(shards, mesh=mesh, in_specs=in_specs, out_specs=out_specs, check_vma=False)
```

```python
import functools

import jax
import jax.numpy as jnp
from jax import lax
from jax.experimental import pallas as pl
from jax.experimental.pallas import tpu as pltpu
from jax.sharding import PartitionSpec as P


def earlier_same(owners):
    slot_count = owners.shape[1]
    same_owner = owners[:, :, None] == owners[:, None, :]
    before = jnp.arange(slot_count)[None, :] < jnp.arange(slot_count)[:, None]
    return jnp.sum(same_owner & before[None, :, :], axis=2)


def pick_rows(wanted, values):
    return jnp.sum(jnp.where(wanted, values[:, None, :], 0), axis=2)


def attend(qblock, keys_use, index_use, live_use, block_start, head_count, head_size, window_len):
    block_len = qblock.shape[0]
    query_rows = qblock.reshape(block_len, head_count, head_size)
    scores = jnp.einsum(
        "thd,kd->thk", query_rows, keys_use[:, :head_size], preferred_element_type=jnp.float32
    ) * head_size ** (-0.5)
    positions = block_start + jnp.arange(block_len)
    allowed = (
        (index_use[None, :] > positions[:, None])
        & (index_use[None, :] <= positions[:, None] + window_len)
        & live_use[None, :]
    )
    scores = jnp.where(allowed[:, None, :], scores, -jnp.inf)
    row_max = jnp.max(scores, axis=2, keepdims=True)
    raw_weights = jnp.exp(scores - row_max)
    row_total = jnp.sum(raw_weights, axis=2, keepdims=True)
    weights = raw_weights.astype(jnp.bfloat16)
    weighted = jnp.einsum(
        "thk,kd->thd", weights, keys_use[:, head_size:], preferred_element_type=jnp.float32
    )
    return (weighted / row_total).astype(jnp.bfloat16).reshape(block_len, head_count * head_size)


def regroup(pieces):
    groups, pages, piece_rows, width = pieces.shape
    return pieces.transpose(1, 0, 2, 3).reshape(pages, groups * piece_rows, width)


def window_kernel(meta, q_ref, cached_hbm, fresh_hbm, out_ref, keys, bias, sems, *, chunk, chunks,
                  split, head_count, head_size, window_len):
    first = meta[0]
    live_from = meta[1]

    def chunk_copy(c, begin):
        j = first + c

        @pl.when(j < split)
        def _():
            cp = pltpu.make_async_copy(
                cached_hbm.at[pl.ds(j * chunk, chunk)], keys.at[pl.ds(c * chunk, chunk)], sems.at[c]
            )
            cp.start() if begin else cp.wait()

        @pl.when(j >= split)
        def _():
            cp = pltpu.make_async_copy(
                fresh_hbm.at[pl.ds((j - split) * chunk, chunk)], keys.at[pl.ds(c * chunk, chunk)], sems.at[c]
            )
            cp.start() if begin else cp.wait()

    for c in range(chunks):
        chunk_copy(c, True)
    rows = lax.broadcasted_iota(jnp.int32, bias.shape, 0)
    cols = lax.broadcasted_iota(jnp.int32, bias.shape, 1)
    allowed = (cols > rows) & (cols <= rows + window_len) & (cols >= live_from)
    bias[...] = jnp.where(allowed, 0.0, -jnp.inf).astype(jnp.float32)
    for c in range(chunks):
        chunk_copy(c, False)
    scale = head_size ** (-0.5)

    def one_head(h, carry):
        lanes = pl.ds(pl.multiple_of(h * head_size, head_size), head_size)
        scores = lax.dot_general(
            q_ref[:, lanes], keys[:, :head_size], (((1,), (1,)), ((), ())),
            preferred_element_type=jnp.float32,
        )
        scores = scores * scale + bias[...]
        row_max = jnp.max(scores, axis=1, keepdims=True)
        raw_weights = jnp.exp(scores - row_max)
        row_total = jnp.sum(raw_weights, axis=1, keepdims=True)
        weighted = jnp.dot(
            raw_weights.astype(jnp.bfloat16), keys[:, head_size:], preferred_element_type=jnp.float32
        )
        out_ref[:, lanes] = (weighted / row_total).astype(out_ref.dtype)
        return carry

    lax.fori_loop(0, head_count, one_head, 0)


def window_attention(query_rows, cached, fresh, first_chunk, live_from, head_count, head_size, window_len):
    tok_rows, width = query_rows.shape
    chunk = tok_rows
    span = window_len + tok_rows
    chunks = span // chunk
    split = cached.shape[0] // chunk
    key_width = cached.shape[1]
    body = functools.partial(
        window_kernel, chunk=chunk, chunks=chunks, split=split, head_count=head_count,
        head_size=head_size, window_len=window_len,
    )
    meta = jnp.stack([first_chunk, live_from]).astype(jnp.int32)
    return pl.pallas_call(
        body,
        out_shape=jax.ShapeDtypeStruct((tok_rows, width), query_rows.dtype),
        grid_spec=pltpu.PrefetchScalarGridSpec(
            num_scalar_prefetch=1,
            grid=(1,),
            in_specs=[
                pl.BlockSpec((tok_rows, width), lambda i, m: (0, 0)),
                pl.BlockSpec(memory_space=pl.ANY),
                pl.BlockSpec(memory_space=pl.ANY),
            ],
            out_specs=pl.BlockSpec((tok_rows, width), lambda i, m: (0, 0)),
            scratch_shapes=[
                pltpu.VMEM((span, key_width), cached.dtype),
                pltpu.VMEM((tok_rows, span), jnp.float32),
                pltpu.SemaphoreType.DMA((chunks,)),
            ],
        ),
        compiler_params=pltpu.CompilerParams(vmem_limit_bytes=48 * 1024 * 1024),
    )(meta, query_rows, cached, fresh)


def shards(queries, new_kv, kv_pool, window_table, append_table, cache_lengths):
    blocks = lax.axis_size("blk")
    groups = lax.axis_size("group")
    my_block = lax.axis_index("blk")
    piece_index = lax.axis_index("group")
    tok_rows = queries.shape[1]
    per_owner = kv_pool.shape[0]
    page_rows = kv_pool.shape[1]
    key_width = kv_pool.shape[2]
    head_size = key_width // 2
    head_count = queries.shape[2] // head_size
    win_pages = window_table.shape[1]
    new_pages = append_table.shape[1]
    win_rows = win_pages * page_rows
    cap_win = (win_pages + blocks - 1) // blocks
    cap_new = (new_pages + blocks - 1) // blocks
    piece_rows = page_rows // groups
    piece_start = piece_index * piece_rows
    fresh_keys = lax.all_gather(new_kv, "group", axis=1, tiled=True)[0]
    append_rows = fresh_keys.shape[0]

    win_owner = window_table // per_owner
    win_rank = earlier_same(win_owner)
    win_wanted = (win_owner == my_block)[:, None, :] & (
        win_rank[:, None, :] == jnp.arange(cap_win)[None, :, None]
    )
    send_ids = pick_rows(win_wanted, window_table % per_owner)
    own_owner = lax.dynamic_index_in_dim(win_owner, my_block, 0, keepdims=False)
    own_rank = lax.dynamic_index_in_dim(win_rank, my_block, 0, keepdims=False)
    arrival = own_owner * cap_win + own_rank
    pool_piece = lax.dynamic_slice_in_dim(kv_pool, piece_start, piece_rows, axis=1)
    outgoing = pool_piece[send_ids.reshape(-1)]
    received = lax.all_to_all(outgoing, "blk", split_axis=0, concat_axis=0, tiled=True)
    cached_piece = received[arrival]
    cached = regroup(lax.all_gather(cached_piece, "group", axis=0, tiled=False))

    new_owner = append_table // per_owner
    new_rank = earlier_same(new_owner)
    mine_owner = lax.dynamic_index_in_dim(new_owner, my_block, 0, keepdims=False)
    mine_rank = lax.dynamic_index_in_dim(new_rank, my_block, 0, keepdims=False)
    dest_wanted = (mine_owner[None, None, :] == jnp.arange(blocks)[:, None, None]) & (
        mine_rank[None, None, :] == jnp.arange(cap_new)[None, :, None]
    )
    page_pick = jnp.sum(jnp.where(dest_wanted, jnp.arange(new_pages)[None, None, :], 0), axis=2)
    fresh_pages = fresh_keys.reshape(new_pages, page_rows, key_width)
    fresh_piece = lax.dynamic_slice_in_dim(fresh_pages, piece_start, piece_rows, axis=1)
    parcels = fresh_piece[page_pick.reshape(-1)]
    arrived = lax.all_to_all(parcels, "blk", split_axis=0, concat_axis=0, tiled=True)
    land_here = new_owner == my_block
    land_source = jnp.argmax(land_here, axis=0)
    land_slot = land_source * cap_new + jnp.take_along_axis(new_rank, land_source[None, :], axis=0)[0]
    land_ids = jnp.take_along_axis(append_table % per_owner, land_source[None, :], axis=0)[0]
    land_live = jnp.any(land_here, axis=0)
    landed = lax.all_gather(arrived[land_slot], "group", axis=0, tiled=False)
    targets = jnp.where(land_live, land_ids, per_owner)
    pool_pieces = kv_pool.reshape(per_owner, groups, piece_rows, key_width)
    new_pool = pool_pieces.at[targets[None, :], jnp.arange(groups)[:, None]].set(landed, mode="drop")
    new_pool = new_pool.reshape(kv_pool.shape)

    own_length = lax.dynamic_index_in_dim(cache_lengths, my_block, 0, keepdims=False)
    filled = jnp.minimum(own_length // page_rows, win_pages)
    first_row = piece_index * tok_rows
    live_from = (win_pages - filled) * page_rows - first_row
    attended = window_attention(
        queries[0], cached.reshape(win_rows, key_width), fresh_keys, piece_index, live_from,
        head_count, head_size, win_rows,
    )
    attn_out = attended.reshape(1, tok_rows, queries.shape[2])
    return (attn_out, new_pool)


def solution(mesh):
    in_specs = (
        P("blk", "group", None),
        P("blk", "group", None),
        P("blk", None, None),
        P(),
        P(),
        P(),
    )
    out_specs = (P("blk", "group", None), P("blk", None, None))
    return jax.shard_map(shards, mesh=mesh, in_specs=in_specs, out_specs=out_specs, check_vma=False)
```

```python
import functools

import jax
import jax.numpy as jnp
from jax import lax
from jax.experimental import pallas as pl
from jax.experimental.pallas import tpu as pltpu
from jax.sharding import PartitionSpec as P


def earlier_same(owners):
    slot_count = owners.shape[1]
    same_owner = owners[:, :, None] == owners[:, None, :]
    before = jnp.arange(slot_count)[None, :] < jnp.arange(slot_count)[:, None]
    return jnp.sum(same_owner & before[None, :, :], axis=2)


def pick_rows(wanted, values):
    return jnp.sum(jnp.where(wanted, values[:, None, :], 0), axis=2)


def attend(qblock, keys_use, index_use, live_use, block_start, head_count, head_size, window_len):
    block_len = qblock.shape[0]
    query_rows = qblock.reshape(block_len, head_count, head_size)
    scores = jnp.einsum(
        "thd,kd->thk", query_rows, keys_use[:, :head_size], preferred_element_type=jnp.float32
    ) * head_size ** (-0.5)
    positions = block_start + jnp.arange(block_len)
    allowed = (
        (index_use[None, :] > positions[:, None])
        & (index_use[None, :] <= positions[:, None] + window_len)
        & live_use[None, :]
    )
    scores = jnp.where(allowed[:, None, :], scores, -jnp.inf)
    row_max = jnp.max(scores, axis=2, keepdims=True)
    raw_weights = jnp.exp(scores - row_max)
    row_total = jnp.sum(raw_weights, axis=2, keepdims=True)
    weights = raw_weights.astype(jnp.bfloat16)
    weighted = jnp.einsum(
        "thk,kd->thd", weights, keys_use[:, head_size:], preferred_element_type=jnp.float32
    )
    return (weighted / row_total).astype(jnp.bfloat16).reshape(block_len, head_count * head_size)


def regroup(pieces):
    groups, pages, piece_rows, width = pieces.shape
    return pieces.transpose(1, 0, 2, 3).reshape(pages, groups * piece_rows, width)


def window_kernel(meta, q_ref, cached_hbm, fresh_hbm, out_ref, keys, bias, sems, *, chunk, chunks,
                  split, head_count, head_size, window_len):
    first = meta[0]
    live_from = meta[1]

    def chunk_copy(c, begin):
        j = first + c

        @pl.when(j < split)
        def _():
            cp = pltpu.make_async_copy(
                cached_hbm.at[pl.ds(j * chunk, chunk)], keys.at[pl.ds(c * chunk, chunk)], sems.at[c]
            )
            cp.start() if begin else cp.wait()

        @pl.when(j >= split)
        def _():
            cp = pltpu.make_async_copy(
                fresh_hbm.at[pl.ds((j - split) * chunk, chunk)], keys.at[pl.ds(c * chunk, chunk)], sems.at[c]
            )
            cp.start() if begin else cp.wait()

    for c in range(chunks):
        chunk_copy(c, True)
    rows = lax.broadcasted_iota(jnp.int32, bias.shape, 0)
    cols = lax.broadcasted_iota(jnp.int32, bias.shape, 1)
    allowed = (cols > rows) & (cols <= rows + window_len) & (cols >= live_from)
    bias[...] = jnp.where(allowed, 0.0, -jnp.inf).astype(jnp.float32)
    for c in range(chunks):
        chunk_copy(c, False)
    scale = head_size ** (-0.5)

    def one_head(h, carry):
        lanes = pl.ds(pl.multiple_of(h * head_size, head_size), head_size)
        scores = lax.dot_general(
            q_ref[:, lanes], keys[:, :head_size], (((1,), (1,)), ((), ())),
            preferred_element_type=jnp.float32,
        )
        scores = scores * scale + bias[...]
        row_max = jnp.max(scores, axis=1, keepdims=True)
        raw_weights = jnp.exp(scores - row_max)
        row_total = jnp.sum(raw_weights, axis=1, keepdims=True)
        weighted = jnp.dot(
            raw_weights.astype(jnp.bfloat16), keys[:, head_size:], preferred_element_type=jnp.float32
        )
        out_ref[:, lanes] = (weighted / row_total).astype(out_ref.dtype)
        return carry

    lax.fori_loop(0, head_count, one_head, 0)


def window_attention(query_rows, cached, fresh, first_chunk, live_from, head_count, head_size, window_len):
    tok_rows, width = query_rows.shape
    chunk = tok_rows
    span = window_len + tok_rows
    chunks = span // chunk
    split = cached.shape[0] // chunk
    key_width = cached.shape[1]
    body = functools.partial(
        window_kernel, chunk=chunk, chunks=chunks, split=split, head_count=head_count,
        head_size=head_size, window_len=window_len,
    )
    meta = jnp.stack([first_chunk, live_from]).astype(jnp.int32)
    return pl.pallas_call(
        body,
        out_shape=jax.ShapeDtypeStruct((tok_rows, width), query_rows.dtype),
        grid_spec=pltpu.PrefetchScalarGridSpec(
            num_scalar_prefetch=1,
            grid=(1,),
            in_specs=[
                pl.BlockSpec((tok_rows, width), lambda i, m: (0, 0)),
                pl.BlockSpec(memory_space=pl.ANY),
                pl.BlockSpec(memory_space=pl.ANY),
            ],
            out_specs=pl.BlockSpec((tok_rows, width), lambda i, m: (0, 0)),
            scratch_shapes=[
                pltpu.VMEM((span, key_width), cached.dtype),
                pltpu.VMEM((tok_rows, span), jnp.float32),
                pltpu.SemaphoreType.DMA((chunks,)),
            ],
        ),
        compiler_params=pltpu.CompilerParams(vmem_limit_bytes=48 * 1024 * 1024),
    )(meta, query_rows, cached, fresh)


def pool_kernel(targets, landed, pool_hbm, out_hbm, sems):
    groups, pages, piece_rows, _ = landed.shape
    for page in range(pages):
        target = targets[page]

        @pl.when(target < pool_hbm.shape[0])
        def _():
            for grp in range(groups):
                pltpu.make_async_copy(
                    landed.at[grp, page], out_hbm.at[target, pl.ds(grp * piece_rows, piece_rows)],
                    sems.at[page, grp],
                ).start()

    for page in range(pages):
        target = targets[page]

        @pl.when(target < pool_hbm.shape[0])
        def _():
            for grp in range(groups):
                pltpu.make_async_copy(
                    landed.at[grp, page], out_hbm.at[target, pl.ds(grp * piece_rows, piece_rows)],
                    sems.at[page, grp],
                ).wait()


def write_pool(kv_pool, landed, targets):
    groups, pages = landed.shape[:2]
    return pl.pallas_call(
        pool_kernel,
        out_shape=jax.ShapeDtypeStruct(kv_pool.shape, kv_pool.dtype),
        grid_spec=pltpu.PrefetchScalarGridSpec(
            num_scalar_prefetch=1,
            grid=(1,),
            in_specs=[
                pl.BlockSpec(landed.shape, lambda i, t: (0, 0, 0, 0)),
                pl.BlockSpec(memory_space=pl.ANY),
            ],
            out_specs=pl.BlockSpec(memory_space=pl.ANY),
            scratch_shapes=[pltpu.SemaphoreType.DMA((pages, groups))],
        ),
        input_output_aliases={2: 0},
    )(targets.astype(jnp.int32), landed, kv_pool)


def shards(queries, new_kv, kv_pool, window_table, append_table, cache_lengths):
    blocks = lax.axis_size("blk")
    groups = lax.axis_size("group")
    my_block = lax.axis_index("blk")
    piece_index = lax.axis_index("group")
    tok_rows = queries.shape[1]
    per_owner = kv_pool.shape[0]
    page_rows = kv_pool.shape[1]
    key_width = kv_pool.shape[2]
    head_size = key_width // 2
    head_count = queries.shape[2] // head_size
    win_pages = window_table.shape[1]
    new_pages = append_table.shape[1]
    win_rows = win_pages * page_rows
    cap_win = (win_pages + blocks - 1) // blocks
    cap_new = (new_pages + blocks - 1) // blocks
    piece_rows = page_rows // groups
    piece_start = piece_index * piece_rows
    fresh_keys = lax.all_gather(new_kv, "group", axis=1, tiled=True)[0]
    append_rows = fresh_keys.shape[0]

    win_owner = window_table // per_owner
    win_rank = earlier_same(win_owner)
    win_wanted = (win_owner == my_block)[:, None, :] & (
        win_rank[:, None, :] == jnp.arange(cap_win)[None, :, None]
    )
    send_ids = pick_rows(win_wanted, window_table % per_owner)
    own_owner = lax.dynamic_index_in_dim(win_owner, my_block, 0, keepdims=False)
    own_rank = lax.dynamic_index_in_dim(win_rank, my_block, 0, keepdims=False)
    arrival = own_owner * cap_win + own_rank
    pool_piece = lax.dynamic_slice_in_dim(kv_pool, piece_start, piece_rows, axis=1)
    outgoing = pool_piece[send_ids.reshape(-1)]
    received = lax.all_to_all(outgoing, "blk", split_axis=0, concat_axis=0, tiled=True)
    cached_piece = received[arrival]
    cached = regroup(lax.all_gather(cached_piece, "group", axis=0, tiled=False))

    new_owner = append_table // per_owner
    new_rank = earlier_same(new_owner)
    mine_owner = lax.dynamic_index_in_dim(new_owner, my_block, 0, keepdims=False)
    mine_rank = lax.dynamic_index_in_dim(new_rank, my_block, 0, keepdims=False)
    dest_wanted = (mine_owner[None, None, :] == jnp.arange(blocks)[:, None, None]) & (
        mine_rank[None, None, :] == jnp.arange(cap_new)[None, :, None]
    )
    page_pick = jnp.sum(jnp.where(dest_wanted, jnp.arange(new_pages)[None, None, :], 0), axis=2)
    fresh_pages = fresh_keys.reshape(new_pages, page_rows, key_width)
    fresh_piece = lax.dynamic_slice_in_dim(fresh_pages, piece_start, piece_rows, axis=1)
    parcels = fresh_piece[page_pick.reshape(-1)]
    arrived = lax.all_to_all(parcels, "blk", split_axis=0, concat_axis=0, tiled=True)
    land_here = new_owner == my_block
    land_source = jnp.argmax(land_here, axis=0)
    land_slot = land_source * cap_new + jnp.take_along_axis(new_rank, land_source[None, :], axis=0)[0]
    land_ids = jnp.take_along_axis(append_table % per_owner, land_source[None, :], axis=0)[0]
    land_live = jnp.any(land_here, axis=0)
    landed = lax.all_gather(arrived[land_slot], "group", axis=0, tiled=False)
    targets = jnp.where(land_live, land_ids, per_owner)
    new_pool = write_pool(kv_pool, landed, targets)

    own_length = lax.dynamic_index_in_dim(cache_lengths, my_block, 0, keepdims=False)
    filled = jnp.minimum(own_length // page_rows, win_pages)
    first_row = piece_index * tok_rows
    live_from = (win_pages - filled) * page_rows - first_row
    attended = window_attention(
        queries[0], cached.reshape(win_rows, key_width), fresh_keys, piece_index, live_from,
        head_count, head_size, win_rows,
    )
    attn_out = attended.reshape(1, tok_rows, queries.shape[2])
    return (attn_out, new_pool)


def solution(mesh):
    in_specs = (
        P("blk", "group", None),
        P("blk", "group", None),
        P("blk", None, None),
        P(),
        P(),
        P(),
    )
    out_specs = (P("blk", "group", None), P("blk", None, None))
    return jax.shard_map(shards, mesh=mesh, in_specs=in_specs, out_specs=out_specs, check_vma=False)
```

```python
import functools

import jax
import jax.numpy as jnp
from jax import lax
from jax.experimental import pallas as pl
from jax.experimental.pallas import tpu as pltpu
from jax.sharding import PartitionSpec as P


def earlier_same(owners):
    slot_count = owners.shape[1]
    same_owner = owners[:, :, None] == owners[:, None, :]
    before = jnp.arange(slot_count)[None, :] < jnp.arange(slot_count)[:, None]
    return jnp.sum(same_owner & before[None, :, :], axis=2)


def pick_rows(wanted, values):
    return jnp.sum(jnp.where(wanted, values[:, None, :], 0), axis=2)


def regroup(pieces):
    groups, pages, piece_rows, width = pieces.shape
    return pieces.transpose(1, 0, 2, 3).reshape(pages, groups * piece_rows, width)


def window_kernel(meta, q_ref, cached_hbm, fresh_hbm, out_ref, keys, bias, sems, *, chunk, chunks,
                  split, head_count, head_size, window_len):
    first = meta[0]
    live_from = meta[1]

    def chunk_copy(c, begin):
        j = first + c

        @pl.when(j < split)
        def _():
            cp = pltpu.make_async_copy(
                cached_hbm.at[pl.ds(j * chunk, chunk)], keys.at[pl.ds(c * chunk, chunk)], sems.at[c]
            )
            cp.start() if begin else cp.wait()

        @pl.when(j >= split)
        def _():
            cp = pltpu.make_async_copy(
                fresh_hbm.at[pl.ds((j - split) * chunk, chunk)], keys.at[pl.ds(c * chunk, chunk)], sems.at[c]
            )
            cp.start() if begin else cp.wait()

    for c in range(chunks):
        chunk_copy(c, True)
    rows = lax.broadcasted_iota(jnp.int32, bias.shape, 0)
    cols = lax.broadcasted_iota(jnp.int32, bias.shape, 1)
    allowed = (cols > rows) & (cols <= rows + window_len) & (cols >= live_from)
    bias[...] = jnp.where(allowed, 0.0, -jnp.inf).astype(jnp.float32)
    for c in range(chunks):
        chunk_copy(c, False)
    scale = head_size ** (-0.5)

    def one_head(h, carry):
        lanes = pl.ds(pl.multiple_of(h * head_size, head_size), head_size)
        scores = lax.dot_general(
            q_ref[:, lanes], keys[:, :head_size], (((1,), (1,)), ((), ())),
            preferred_element_type=jnp.float32,
        )
        scores = scores * scale + bias[...]
        row_max = jnp.max(scores, axis=1, keepdims=True)
        raw_weights = jnp.exp(scores - row_max)
        row_total = jnp.sum(raw_weights, axis=1, keepdims=True)
        weighted = jnp.dot(
            raw_weights.astype(jnp.bfloat16), keys[:, head_size:], preferred_element_type=jnp.float32
        )
        out_ref[:, lanes] = (weighted / row_total).astype(out_ref.dtype)
        return carry

    lax.fori_loop(0, head_count, one_head, 0)


def window_attention(query_rows, cached, fresh, first_chunk, live_from, head_count, head_size, window_len):
    tok_rows, width = query_rows.shape
    chunk = tok_rows
    span = window_len + tok_rows
    chunks = span // chunk
    split = cached.shape[0] // chunk
    key_width = cached.shape[1]
    body = functools.partial(
        window_kernel, chunk=chunk, chunks=chunks, split=split, head_count=head_count,
        head_size=head_size, window_len=window_len,
    )
    meta = jnp.stack([first_chunk, live_from]).astype(jnp.int32)
    return pl.pallas_call(
        body,
        out_shape=jax.ShapeDtypeStruct((tok_rows, width), query_rows.dtype),
        grid_spec=pltpu.PrefetchScalarGridSpec(
            num_scalar_prefetch=1,
            grid=(1,),
            in_specs=[
                pl.BlockSpec((tok_rows, width), lambda i, m: (0, 0)),
                pl.BlockSpec(memory_space=pl.ANY),
                pl.BlockSpec(memory_space=pl.ANY),
            ],
            out_specs=pl.BlockSpec((tok_rows, width), lambda i, m: (0, 0)),
            scratch_shapes=[
                pltpu.VMEM((span, key_width), cached.dtype),
                pltpu.VMEM((tok_rows, span), jnp.float32),
                pltpu.SemaphoreType.DMA((chunks,)),
            ],
        ),
        compiler_params=pltpu.CompilerParams(vmem_limit_bytes=48 * 1024 * 1024),
    )(meta, query_rows, cached, fresh)


def pool_kernel(targets, landed, pool_hbm, out_hbm, sems):
    groups, pages, piece_rows, _ = landed.shape
    for page in range(pages):
        target = targets[page]

        @pl.when(target < pool_hbm.shape[0])
        def _():
            for grp in range(groups):
                pltpu.make_async_copy(
                    landed.at[grp, page], out_hbm.at[target, pl.ds(grp * piece_rows, piece_rows)],
                    sems.at[page, grp],
                ).start()

    for page in range(pages):
        target = targets[page]

        @pl.when(target < pool_hbm.shape[0])
        def _():
            for grp in range(groups):
                pltpu.make_async_copy(
                    landed.at[grp, page], out_hbm.at[target, pl.ds(grp * piece_rows, piece_rows)],
                    sems.at[page, grp],
                ).wait()


def copy_kernel(src_ref, dst_ref):
    dst_ref[...] = src_ref[...]


def copy_pool(kv_pool):
    pages = kv_pool.shape[0]
    block = (8,) + kv_pool.shape[1:]
    return pl.pallas_call(
        copy_kernel,
        out_shape=jax.ShapeDtypeStruct(kv_pool.shape, kv_pool.dtype),
        grid=(pages // 8,),
        in_specs=[pl.BlockSpec(block, lambda i: (i, 0, 0))],
        out_specs=pl.BlockSpec(block, lambda i: (i, 0, 0)),
    )(kv_pool)


def write_pool(kv_pool, landed, targets):
    groups, pages = landed.shape[:2]
    return pl.pallas_call(
        pool_kernel,
        out_shape=jax.ShapeDtypeStruct(kv_pool.shape, kv_pool.dtype),
        grid_spec=pltpu.PrefetchScalarGridSpec(
            num_scalar_prefetch=1,
            grid=(1,),
            in_specs=[
                pl.BlockSpec(landed.shape, lambda i, t: (0, 0, 0, 0)),
                pl.BlockSpec(memory_space=pl.ANY),
            ],
            out_specs=pl.BlockSpec(memory_space=pl.ANY),
            scratch_shapes=[pltpu.SemaphoreType.DMA((pages, groups))],
        ),
        input_output_aliases={2: 0},
    )(targets.astype(jnp.int32), landed, kv_pool)


def shards_body(queries, new_kv, kv_pool, window_table, append_table, cache_lengths):
    blocks = lax.axis_size("blk")
    groups = lax.axis_size("group")
    my_block = lax.axis_index("blk")
    piece_index = lax.axis_index("group")
    tok_rows = queries.shape[1]
    per_owner = kv_pool.shape[0]
    page_rows = kv_pool.shape[1]
    key_width = kv_pool.shape[2]
    head_size = key_width // 2
    head_count = queries.shape[2] // head_size
    win_pages = window_table.shape[1]
    new_pages = append_table.shape[1]
    win_rows = win_pages * page_rows
    cap_win = (win_pages + blocks - 1) // blocks
    cap_new = (new_pages + blocks - 1) // blocks
    piece_rows = page_rows // groups
    piece_start = piece_index * piece_rows
    fresh_keys = lax.all_gather(new_kv, "group", axis=1, tiled=True)[0]

    win_owner = window_table // per_owner
    win_rank = earlier_same(win_owner)
    win_wanted = (win_owner == my_block)[:, None, :] & (
        win_rank[:, None, :] == jnp.arange(cap_win)[None, :, None]
    )
    send_ids = pick_rows(win_wanted, window_table % per_owner)
    own_owner = lax.dynamic_index_in_dim(win_owner, my_block, 0, keepdims=False)
    own_rank = lax.dynamic_index_in_dim(win_rank, my_block, 0, keepdims=False)
    arrival = own_owner * cap_win + own_rank
    pool_piece = lax.dynamic_slice_in_dim(kv_pool, piece_start, piece_rows, axis=1)
    outgoing = pool_piece[send_ids.reshape(-1)]
    received = lax.all_to_all(outgoing, "blk", split_axis=0, concat_axis=0, tiled=True)
    pool_out = copy_pool(kv_pool)
    cached_piece = received[arrival]
    cached = regroup(lax.all_gather(cached_piece, "group", axis=0, tiled=False))

    new_owner = append_table // per_owner
    new_rank = earlier_same(new_owner)
    mine_owner = lax.dynamic_index_in_dim(new_owner, my_block, 0, keepdims=False)
    mine_rank = lax.dynamic_index_in_dim(new_rank, my_block, 0, keepdims=False)
    dest_wanted = (mine_owner[None, None, :] == jnp.arange(blocks)[:, None, None]) & (
        mine_rank[None, None, :] == jnp.arange(cap_new)[None, :, None]
    )
    page_pick = jnp.sum(jnp.where(dest_wanted, jnp.arange(new_pages)[None, None, :], 0), axis=2)
    fresh_pages = fresh_keys.reshape(new_pages, page_rows, key_width)
    fresh_piece = lax.dynamic_slice_in_dim(fresh_pages, piece_start, piece_rows, axis=1)
    parcels = fresh_piece[page_pick.reshape(-1)]
    arrived = lax.all_to_all(parcels, "blk", split_axis=0, concat_axis=0, tiled=True)
    land_here = new_owner == my_block
    land_source = jnp.argmax(land_here, axis=0)
    land_slot = land_source * cap_new + jnp.take_along_axis(new_rank, land_source[None, :], axis=0)[0]
    land_ids = jnp.take_along_axis(append_table % per_owner, land_source[None, :], axis=0)[0]
    land_live = jnp.any(land_here, axis=0)
    landed = lax.all_gather(arrived[land_slot], "group", axis=0, tiled=False)
    targets = jnp.where(land_live, land_ids, per_owner)
    new_pool = write_pool(pool_out, landed, targets)

    own_length = lax.dynamic_index_in_dim(cache_lengths, my_block, 0, keepdims=False)
    filled = jnp.minimum(own_length // page_rows, win_pages)
    first_row = piece_index * tok_rows
    live_from = (win_pages - filled) * page_rows - first_row
    attended = window_attention(
        queries[0], cached.reshape(win_rows, key_width), fresh_keys, piece_index, live_from,
        head_count, head_size, win_rows,
    )
    attn_out = attended.reshape(1, tok_rows, queries.shape[2])
    return (attn_out, new_pool)


def solution(mesh):
    in_specs = (
        P("blk", "group", None),
        P("blk", "group", None),
        P("blk", None, None),
        P(),
        P(),
        P(),
    )
    out_specs = (P("blk", "group", None), P("blk", None, None))
    return jax.shard_map(shards_body, mesh=mesh, in_specs=in_specs, out_specs=out_specs, check_vma=False)
```

```python
import functools

import jax
import jax.numpy as jnp
from jax import lax
from jax.experimental import pallas as pl
from jax.experimental.pallas import tpu as pltpu
from jax.sharding import PartitionSpec as P


def earlier_same(owners):
    slot_count = owners.shape[1]
    same_owner = owners[:, :, None] == owners[:, None, :]
    before = jnp.arange(slot_count)[None, :] < jnp.arange(slot_count)[:, None]
    return jnp.sum(same_owner & before[None, :, :], axis=2)


def pick_rows(wanted, values):
    return jnp.sum(jnp.where(wanted, values[:, None, :], 0), axis=2)


def regroup(pieces):
    groups, pages, piece_rows, width = pieces.shape
    return pieces.transpose(1, 0, 2, 3).reshape(pages, groups * piece_rows, width)


def window_kernel(meta, q_ref, cached_hbm, fresh_hbm, out_ref, keys, bias, sems, *, chunk, chunks,
                  split, head_count, head_size, window_len):
    first = meta[0]
    live_from = meta[1]

    def chunk_copy(c, begin):
        j = first + c

        @pl.when(j < split)
        def _():
            cp = pltpu.make_async_copy(
                cached_hbm.at[pl.ds(j * chunk, chunk)], keys.at[pl.ds(c * chunk, chunk)], sems.at[c]
            )
            cp.start() if begin else cp.wait()

        @pl.when(j >= split)
        def _():
            cp = pltpu.make_async_copy(
                fresh_hbm.at[pl.ds((j - split) * chunk, chunk)], keys.at[pl.ds(c * chunk, chunk)], sems.at[c]
            )
            cp.start() if begin else cp.wait()

    for c in range(chunks):
        chunk_copy(c, True)
    rows = lax.broadcasted_iota(jnp.int32, bias.shape, 0)
    cols = lax.broadcasted_iota(jnp.int32, bias.shape, 1)
    allowed = (cols > rows) & (cols <= rows + window_len) & (cols >= live_from)
    bias[...] = jnp.where(allowed, 0.0, -jnp.inf).astype(jnp.float32)
    for c in range(chunks):
        chunk_copy(c, False)
    scale = head_size ** (-0.5)

    def one_head(h, carry):
        lanes = pl.ds(pl.multiple_of(h * head_size, head_size), head_size)
        scores = lax.dot_general(
            q_ref[:, lanes], keys[:, :head_size], (((1,), (1,)), ((), ())),
            preferred_element_type=jnp.float32,
        )
        scores = scores * scale + bias[...]
        row_max = jnp.max(scores, axis=1, keepdims=True)
        raw_weights = jnp.exp(scores - row_max)
        row_total = jnp.sum(raw_weights, axis=1, keepdims=True)
        weighted = jnp.dot(
            raw_weights.astype(jnp.bfloat16), keys[:, head_size:], preferred_element_type=jnp.float32
        )
        out_ref[:, lanes] = (weighted / row_total).astype(out_ref.dtype)
        return carry

    lax.fori_loop(0, head_count, one_head, 0)


def window_attention(query_rows, cached, fresh, first_chunk, live_from, head_count, head_size, window_len):
    tok_rows, width = query_rows.shape
    chunk = tok_rows
    span = window_len + tok_rows
    chunks = span // chunk
    split = cached.shape[0] // chunk
    key_width = cached.shape[1]
    body = functools.partial(
        window_kernel, chunk=chunk, chunks=chunks, split=split, head_count=head_count,
        head_size=head_size, window_len=window_len,
    )
    meta = jnp.stack([first_chunk, live_from]).astype(jnp.int32)
    return pl.pallas_call(
        body,
        out_shape=jax.ShapeDtypeStruct((tok_rows, width), query_rows.dtype),
        grid_spec=pltpu.PrefetchScalarGridSpec(
            num_scalar_prefetch=1,
            grid=(1,),
            in_specs=[
                pl.BlockSpec((tok_rows, width), lambda i, m: (0, 0)),
                pl.BlockSpec(memory_space=pl.ANY),
                pl.BlockSpec(memory_space=pl.ANY),
            ],
            out_specs=pl.BlockSpec((tok_rows, width), lambda i, m: (0, 0)),
            scratch_shapes=[
                pltpu.VMEM((span, key_width), cached.dtype),
                pltpu.VMEM((tok_rows, span), jnp.float32),
                pltpu.SemaphoreType.DMA((chunks,)),
            ],
        ),
        compiler_params=pltpu.CompilerParams(vmem_limit_bytes=48 * 1024 * 1024),
    )(meta, query_rows, cached, fresh)


def pool_kernel(targets, landed_hbm, pool_hbm, out_hbm, staged, in_sems, out_sems):
    groups, pages, piece_rows, _ = landed_hbm.shape
    for grp in range(groups):
        pltpu.make_async_copy(landed_hbm.at[grp], staged.at[grp], in_sems.at[grp]).start()

    def each_target(grp, begin):
        for page in range(pages):
            target = targets[page]

            @pl.when(target < pool_hbm.shape[0])
            def _():
                cp = pltpu.make_async_copy(
                    staged.at[grp, page], out_hbm.at[target, pl.ds(grp * piece_rows, piece_rows)],
                    out_sems.at[page, grp],
                )
                cp.start() if begin else cp.wait()

    for grp in range(groups):
        pltpu.make_async_copy(landed_hbm.at[grp], staged.at[grp], in_sems.at[grp]).wait()
        each_target(grp, True)
    for grp in range(groups):
        each_target(grp, False)


def write_pool(kv_pool, landed, targets):
    groups, pages = landed.shape[:2]
    return pl.pallas_call(
        pool_kernel,
        out_shape=jax.ShapeDtypeStruct(kv_pool.shape, kv_pool.dtype),
        grid_spec=pltpu.PrefetchScalarGridSpec(
            num_scalar_prefetch=1,
            grid=(1,),
            in_specs=[pl.BlockSpec(memory_space=pl.ANY), pl.BlockSpec(memory_space=pl.ANY)],
            out_specs=pl.BlockSpec(memory_space=pl.ANY),
            scratch_shapes=[
                pltpu.VMEM(landed.shape, landed.dtype),
                pltpu.SemaphoreType.DMA((groups,)),
                pltpu.SemaphoreType.DMA((pages, groups)),
            ],
        ),
        input_output_aliases={2: 0},
    )(targets.astype(jnp.int32), landed, kv_pool)


def copy_kernel(src_ref, dst_ref):
    dst_ref[...] = src_ref[...]


def copy_pool(kv_pool):
    pages = kv_pool.shape[0]
    block = (8,) + kv_pool.shape[1:]
    return pl.pallas_call(
        copy_kernel,
        out_shape=jax.ShapeDtypeStruct(kv_pool.shape, kv_pool.dtype),
        grid=(pages // 8,),
        in_specs=[pl.BlockSpec(block, lambda i: (i, 0, 0))],
        out_specs=pl.BlockSpec(block, lambda i: (i, 0, 0)),
    )(kv_pool)


def shards_body(queries, new_kv, kv_pool, window_table, append_table, cache_lengths):
    blocks = lax.axis_size("blk")
    groups = lax.axis_size("group")
    my_block = lax.axis_index("blk")
    piece_index = lax.axis_index("group")
    tok_rows = queries.shape[1]
    per_owner = kv_pool.shape[0]
    page_rows = kv_pool.shape[1]
    key_width = kv_pool.shape[2]
    head_size = key_width // 2
    head_count = queries.shape[2] // head_size
    win_pages = window_table.shape[1]
    new_pages = append_table.shape[1]
    win_rows = win_pages * page_rows
    cap_win = (win_pages + blocks - 1) // blocks
    cap_new = (new_pages + blocks - 1) // blocks
    piece_rows = page_rows // groups
    piece_start = piece_index * piece_rows
    fresh_keys = lax.all_gather(new_kv, "group", axis=1, tiled=True)[0]

    win_owner = window_table // per_owner
    win_rank = earlier_same(win_owner)
    win_wanted = (win_owner == my_block)[:, None, :] & (
        win_rank[:, None, :] == jnp.arange(cap_win)[None, :, None]
    )
    send_ids = pick_rows(win_wanted, window_table % per_owner)
    own_owner = lax.dynamic_index_in_dim(win_owner, my_block, 0, keepdims=False)
    own_rank = lax.dynamic_index_in_dim(win_rank, my_block, 0, keepdims=False)
    arrival = own_owner * cap_win + own_rank
    pool_piece = lax.dynamic_slice_in_dim(kv_pool, piece_start, piece_rows, axis=1)
    outgoing = pool_piece[send_ids.reshape(-1)]
    received = lax.all_to_all(outgoing, "blk", split_axis=0, concat_axis=0, tiled=True)
    pool_out = copy_pool(kv_pool)
    cached_piece = received[arrival]
    cached = regroup(lax.all_gather(cached_piece, "group", axis=0, tiled=False))

    new_owner = append_table // per_owner
    new_rank = earlier_same(new_owner)
    mine_owner = lax.dynamic_index_in_dim(new_owner, my_block, 0, keepdims=False)
    mine_rank = lax.dynamic_index_in_dim(new_rank, my_block, 0, keepdims=False)
    dest_wanted = (mine_owner[None, None, :] == jnp.arange(blocks)[:, None, None]) & (
        mine_rank[None, None, :] == jnp.arange(cap_new)[None, :, None]
    )
    page_pick = jnp.sum(jnp.where(dest_wanted, jnp.arange(new_pages)[None, None, :], 0), axis=2)
    fresh_pages = fresh_keys.reshape(new_pages, page_rows, key_width)
    fresh_piece = lax.dynamic_slice_in_dim(fresh_pages, piece_start, piece_rows, axis=1)
    parcels = fresh_piece[page_pick.reshape(-1)]
    arrived = lax.all_to_all(parcels, "blk", split_axis=0, concat_axis=0, tiled=True)
    land_here = new_owner == my_block
    land_source = jnp.argmax(land_here, axis=0)
    land_slot = land_source * cap_new + jnp.take_along_axis(new_rank, land_source[None, :], axis=0)[0]
    land_ids = jnp.take_along_axis(append_table % per_owner, land_source[None, :], axis=0)[0]
    land_live = jnp.any(land_here, axis=0)
    landed = lax.all_gather(arrived[land_slot], "group", axis=0, tiled=False)
    targets = jnp.where(land_live, land_ids, per_owner)
    new_pool = write_pool(pool_out, landed, targets)

    own_length = lax.dynamic_index_in_dim(cache_lengths, my_block, 0, keepdims=False)
    filled = jnp.minimum(own_length // page_rows, win_pages)
    first_row = piece_index * tok_rows
    live_from = (win_pages - filled) * page_rows - first_row
    attended = window_attention(
        queries[0], cached.reshape(win_rows, key_width), fresh_keys, piece_index, live_from,
        head_count, head_size, win_rows,
    )
    attn_out = attended.reshape(1, tok_rows, queries.shape[2])
    return (attn_out, new_pool)


def solution(mesh):
    in_specs = (
        P("blk", "group", None),
        P("blk", "group", None),
        P("blk", None, None),
        P(),
        P(),
        P(),
    )
    out_specs = (P("blk", "group", None), P("blk", None, None))
    return jax.shard_map(shards_body, mesh=mesh, in_specs=in_specs, out_specs=out_specs, check_vma=False)
```

```python
import functools

import jax
import jax.numpy as jnp
from jax import lax
from jax.experimental import pallas as pl
from jax.experimental.pallas import tpu as pltpu
from jax.sharding import PartitionSpec as P


def earlier_same(owners):
    slot_count = owners.shape[1]
    same_owner = owners[:, :, None] == owners[:, None, :]
    before = jnp.arange(slot_count)[None, :] < jnp.arange(slot_count)[:, None]
    return jnp.sum(same_owner & before[None, :, :], axis=2)


def pick_rows(wanted, values):
    return jnp.sum(jnp.where(wanted, values[:, None, :], 0), axis=2)


def regroup(pieces):
    groups, pages, piece_rows, width = pieces.shape
    return pieces.transpose(1, 0, 2, 3).reshape(pages, groups * piece_rows, width)


def window_kernel(meta, q_ref, cached_hbm, fresh_hbm, out_ref, keys, bias, sems, *, chunk, chunks,
                  split, head_count, head_size, window_len):
    first = meta[0]
    live_from = meta[1]

    def chunk_copy(c, begin):
        j = first + c

        @pl.when(j < split)
        def _():
            cp = pltpu.make_async_copy(
                cached_hbm.at[pl.ds(j * chunk, chunk)], keys.at[pl.ds(c * chunk, chunk)], sems.at[c]
            )
            cp.start() if begin else cp.wait()

        @pl.when(j >= split)
        def _():
            cp = pltpu.make_async_copy(
                fresh_hbm.at[pl.ds((j - split) * chunk, chunk)], keys.at[pl.ds(c * chunk, chunk)], sems.at[c]
            )
            cp.start() if begin else cp.wait()

    for c in range(chunks):
        chunk_copy(c, True)
    rows = lax.broadcasted_iota(jnp.int32, bias.shape, 0)
    cols = lax.broadcasted_iota(jnp.int32, bias.shape, 1)
    allowed = (cols > rows) & (cols <= rows + window_len) & (cols >= live_from)
    bias[...] = jnp.where(allowed, 0.0, -jnp.inf).astype(jnp.float32)
    for c in range(chunks):
        chunk_copy(c, False)
    scale = head_size ** (-0.5)

    def one_head(h, carry):
        lanes = pl.ds(pl.multiple_of(h * head_size, head_size), head_size)
        scores = lax.dot_general(
            q_ref[:, lanes], keys[:, :head_size], (((1,), (1,)), ((), ())),
            preferred_element_type=jnp.float32,
        )
        scores = scores * scale + bias[...]
        row_max = jnp.max(scores, axis=1, keepdims=True)
        raw_weights = jnp.exp(scores - row_max)
        row_total = jnp.sum(raw_weights, axis=1, keepdims=True)
        weighted = jnp.dot(
            raw_weights.astype(jnp.bfloat16), keys[:, head_size:], preferred_element_type=jnp.float32
        )
        out_ref[:, lanes] = (weighted / row_total).astype(out_ref.dtype)
        return carry

    lax.fori_loop(0, head_count, one_head, 0)


def window_attention(query_rows, cached, fresh, first_chunk, live_from, head_count, head_size, window_len):
    tok_rows, width = query_rows.shape
    chunk = tok_rows
    span = window_len + tok_rows
    chunks = span // chunk
    split = cached.shape[0] // chunk
    key_width = cached.shape[1]
    body = functools.partial(
        window_kernel, chunk=chunk, chunks=chunks, split=split, head_count=head_count,
        head_size=head_size, window_len=window_len,
    )
    meta = jnp.stack([first_chunk, live_from]).astype(jnp.int32)
    return pl.pallas_call(
        body,
        out_shape=jax.ShapeDtypeStruct((tok_rows, width), query_rows.dtype),
        grid_spec=pltpu.PrefetchScalarGridSpec(
            num_scalar_prefetch=1,
            grid=(1,),
            in_specs=[
                pl.BlockSpec((tok_rows, width), lambda i, m: (0, 0)),
                pl.BlockSpec(memory_space=pl.ANY),
                pl.BlockSpec(memory_space=pl.ANY),
            ],
            out_specs=pl.BlockSpec((tok_rows, width), lambda i, m: (0, 0)),
            scratch_shapes=[
                pltpu.VMEM((span, key_width), cached.dtype),
                pltpu.VMEM((tok_rows, span), jnp.float32),
                pltpu.SemaphoreType.DMA((chunks,)),
            ],
        ),
        compiler_params=pltpu.CompilerParams(vmem_limit_bytes=48 * 1024 * 1024),
    )(meta, query_rows, cached, fresh)


def pool_kernel(targets, landed_hbm, pool_hbm, out_hbm, staged, in_sems, out_sems):
    groups, pages, piece_rows, _ = landed_hbm.shape
    for grp in range(groups):
        pltpu.make_async_copy(landed_hbm.at[grp], staged.at[grp], in_sems.at[grp]).start()

    def each_target(grp, begin):
        for page in range(pages):
            target = targets[page]

            @pl.when(target < pool_hbm.shape[0])
            def _():
                cp = pltpu.make_async_copy(
                    staged.at[grp, page], out_hbm.at[target, pl.ds(grp * piece_rows, piece_rows)],
                    out_sems.at[page, grp],
                )
                cp.start() if begin else cp.wait()

    for grp in range(groups):
        pltpu.make_async_copy(landed_hbm.at[grp], staged.at[grp], in_sems.at[grp]).wait()
        each_target(grp, True)
    for grp in range(groups):
        each_target(grp, False)


def write_pool(kv_pool, landed, targets):
    groups, pages = landed.shape[:2]
    return pl.pallas_call(
        pool_kernel,
        out_shape=jax.ShapeDtypeStruct(kv_pool.shape, kv_pool.dtype),
        grid_spec=pltpu.PrefetchScalarGridSpec(
            num_scalar_prefetch=1,
            grid=(1,),
            in_specs=[pl.BlockSpec(memory_space=pl.ANY), pl.BlockSpec(memory_space=pl.ANY)],
            out_specs=pl.BlockSpec(memory_space=pl.ANY),
            scratch_shapes=[
                pltpu.VMEM(landed.shape, landed.dtype),
                pltpu.SemaphoreType.DMA((groups,)),
                pltpu.SemaphoreType.DMA((pages, groups)),
            ],
        ),
        input_output_aliases={2: 0},
    )(targets.astype(jnp.int32), landed, kv_pool)


def copy_kernel(src_ref, dst_ref):
    dst_ref[...] = src_ref[...]


def copy_pool(kv_pool):
    pages = kv_pool.shape[0]
    block = (8,) + kv_pool.shape[1:]
    return pl.pallas_call(
        copy_kernel,
        out_shape=jax.ShapeDtypeStruct(kv_pool.shape, kv_pool.dtype),
        grid=(pages // 8,),
        in_specs=[pl.BlockSpec(block, lambda i: (i, 0, 0))],
        out_specs=pl.BlockSpec(block, lambda i: (i, 0, 0)),
    )(kv_pool)


def shards_body(queries, new_kv, kv_pool, window_table, append_table, cache_lengths):
    blocks = lax.axis_size("blk")
    groups = lax.axis_size("group")
    my_block = lax.axis_index("blk")
    piece_index = lax.axis_index("group")
    tok_rows = queries.shape[1]
    per_owner = kv_pool.shape[0]
    page_rows = kv_pool.shape[1]
    key_width = kv_pool.shape[2]
    head_size = key_width // 2
    head_count = queries.shape[2] // head_size
    win_pages = window_table.shape[1]
    new_pages = append_table.shape[1]
    win_rows = win_pages * page_rows
    cap_win = (win_pages + blocks - 1) // blocks
    cap_new = (new_pages + blocks - 1) // blocks
    piece_rows = page_rows // groups
    piece_start = piece_index * piece_rows
    fresh_keys = lax.all_gather(new_kv, "group", axis=1, tiled=True)[0]

    win_owner = window_table // per_owner
    win_rank = earlier_same(win_owner)
    win_wanted = (win_owner == my_block)[:, None, :] & (
        win_rank[:, None, :] == jnp.arange(cap_win)[None, :, None]
    )
    send_ids = pick_rows(win_wanted, window_table % per_owner)
    own_owner = lax.dynamic_index_in_dim(win_owner, my_block, 0, keepdims=False)
    own_rank = lax.dynamic_index_in_dim(win_rank, my_block, 0, keepdims=False)
    arrival = own_owner * cap_win + own_rank
    pool_piece = lax.dynamic_slice_in_dim(kv_pool, piece_start, piece_rows, axis=1)
    outgoing = pool_piece[send_ids.reshape(-1)]
    received = lax.all_to_all(outgoing, "blk", split_axis=0, concat_axis=0, tiled=True)
    pool_out = copy_pool(kv_pool)
    cached_piece = received[arrival]
    cached = regroup(lax.all_gather(cached_piece, "group", axis=0, tiled=False))

    new_owner = append_table // per_owner
    new_rank = earlier_same(new_owner)
    mine_owner = lax.dynamic_index_in_dim(new_owner, my_block, 0, keepdims=False)
    mine_rank = lax.dynamic_index_in_dim(new_rank, my_block, 0, keepdims=False)
    dest_wanted = (mine_owner[None, None, :] == jnp.arange(blocks)[:, None, None]) & (
        mine_rank[None, None, :] == jnp.arange(cap_new)[None, :, None]
    )
    page_pick = jnp.sum(jnp.where(dest_wanted, jnp.arange(new_pages)[None, None, :], 0), axis=2)
    own_pages = new_kv[0].reshape(-1, groups, piece_rows, key_width)
    shifted = [lax.dynamic_index_in_dim(own_pages, piece_index, 1, keepdims=False)]
    for shift in range(1, groups):
        outgoing_piece = lax.dynamic_index_in_dim(
            own_pages, (piece_index + shift) % groups, 1, keepdims=False
        )
        shifted.append(lax.ppermute(
            outgoing_piece, "group", [(i, (i + shift) % groups) for i in range(groups)]
        ))
    by_shift = jnp.stack(shifted)
    fresh_piece = by_shift[(piece_index - jnp.arange(groups)) % groups].reshape(
        new_pages, piece_rows, key_width
    )
    parcels = fresh_piece[page_pick.reshape(-1)]
    arrived = lax.all_to_all(parcels, "blk", split_axis=0, concat_axis=0, tiled=True)
    land_here = new_owner == my_block
    land_source = jnp.argmax(land_here, axis=0)
    land_slot = land_source * cap_new + jnp.take_along_axis(new_rank, land_source[None, :], axis=0)[0]
    land_ids = jnp.take_along_axis(append_table % per_owner, land_source[None, :], axis=0)[0]
    land_live = jnp.any(land_here, axis=0)
    landed = lax.all_gather(arrived[land_slot], "group", axis=0, tiled=False)
    targets = jnp.where(land_live, land_ids, per_owner)
    new_pool = write_pool(pool_out, landed, targets)

    own_length = lax.dynamic_index_in_dim(cache_lengths, my_block, 0, keepdims=False)
    filled = jnp.minimum(own_length // page_rows, win_pages)
    first_row = piece_index * tok_rows
    live_from = (win_pages - filled) * page_rows - first_row
    attended = window_attention(
        queries[0], cached.reshape(win_rows, key_width), fresh_keys, piece_index, live_from,
        head_count, head_size, win_rows,
    )
    attn_out = attended.reshape(1, tok_rows, queries.shape[2])
    return (attn_out, new_pool)


def solution(mesh):
    in_specs = (
        P("blk", "group", None),
        P("blk", "group", None),
        P("blk", None, None),
        P(),
        P(),
        P(),
    )
    out_specs = (P("blk", "group", None), P("blk", None, None))
    return jax.shard_map(shards_body, mesh=mesh, in_specs=in_specs, out_specs=out_specs, check_vma=False)
```

```python
import functools

import jax
import jax.numpy as jnp
from jax import lax
from jax.experimental import pallas as pl
from jax.experimental.pallas import tpu as pltpu
from jax.sharding import PartitionSpec as P


def earlier_same(owners):
    slot_count = owners.shape[1]
    same_owner = owners[:, :, None] == owners[:, None, :]
    before = jnp.arange(slot_count)[None, :] < jnp.arange(slot_count)[:, None]
    return jnp.sum(same_owner & before[None, :, :], axis=2)


def pick_rows(wanted, values):
    return jnp.sum(jnp.where(wanted, values[:, None, :], 0), axis=2)


def window_kernel(meta, q_ref, cached_hbm, fresh_hbm, out_ref, keys, bias, sems, *, chunk, chunks,
                  split, head_count, head_size, window_len):
    first = meta[0]
    live_from = meta[1]

    def chunk_copy(c, begin):
        j = first + c

        @pl.when(j < split)
        def _():
            cp = pltpu.make_async_copy(
                cached_hbm.at[pl.ds(j * chunk, chunk)], keys.at[pl.ds(c * chunk, chunk)], sems.at[c]
            )
            cp.start() if begin else cp.wait()

        @pl.when(j >= split)
        def _():
            cp = pltpu.make_async_copy(
                fresh_hbm.at[pl.ds((j - split) * chunk, chunk)], keys.at[pl.ds(c * chunk, chunk)], sems.at[c]
            )
            cp.start() if begin else cp.wait()

    for c in range(chunks):
        chunk_copy(c, True)
    rows = lax.broadcasted_iota(jnp.int32, bias.shape, 0)
    cols = lax.broadcasted_iota(jnp.int32, bias.shape, 1)
    allowed = (cols > rows) & (cols <= rows + window_len) & (cols >= live_from)
    bias[...] = jnp.where(allowed, 0.0, -jnp.inf).astype(jnp.float32)
    for c in range(chunks):
        chunk_copy(c, False)
    scale = head_size ** (-0.5)

    def one_head(h, carry):
        lanes = pl.ds(pl.multiple_of(h * head_size, head_size), head_size)
        scores = lax.dot_general(
            q_ref[:, lanes], keys[:, :head_size], (((1,), (1,)), ((), ())),
            preferred_element_type=jnp.float32,
        )
        scores = scores * scale + bias[...]
        row_max = jnp.max(scores, axis=1, keepdims=True)
        raw_weights = jnp.exp(scores - row_max)
        row_total = jnp.sum(raw_weights, axis=1, keepdims=True)
        weighted = jnp.dot(
            raw_weights.astype(jnp.bfloat16), keys[:, head_size:], preferred_element_type=jnp.float32
        )
        out_ref[:, lanes] = (weighted / row_total).astype(out_ref.dtype)
        return carry

    lax.fori_loop(0, head_count, one_head, 0)


def window_attention(query_rows, cached, fresh, first_chunk, live_from, head_count, head_size, window_len):
    tok_rows, width = query_rows.shape
    chunk = tok_rows
    span = window_len + tok_rows
    chunks = span // chunk
    split = cached.shape[0] // chunk
    key_width = cached.shape[1]
    body = functools.partial(
        window_kernel, chunk=chunk, chunks=chunks, split=split, head_count=head_count,
        head_size=head_size, window_len=window_len,
    )
    meta = jnp.stack([first_chunk, live_from]).astype(jnp.int32)
    return pl.pallas_call(
        body,
        out_shape=jax.ShapeDtypeStruct((tok_rows, width), query_rows.dtype),
        grid_spec=pltpu.PrefetchScalarGridSpec(
            num_scalar_prefetch=1,
            grid=(1,),
            in_specs=[
                pl.BlockSpec((tok_rows, width), lambda i, m: (0, 0)),
                pl.BlockSpec(memory_space=pl.ANY),
                pl.BlockSpec(memory_space=pl.ANY),
            ],
            out_specs=pl.BlockSpec((tok_rows, width), lambda i, m: (0, 0)),
            scratch_shapes=[
                pltpu.VMEM((span, key_width), cached.dtype),
                pltpu.VMEM((tok_rows, span), jnp.float32),
                pltpu.SemaphoreType.DMA((chunks,)),
            ],
        ),
        compiler_params=pltpu.CompilerParams(vmem_limit_bytes=48 * 1024 * 1024),
    )(meta, query_rows, cached, fresh)


def pool_kernel(targets, landed_hbm, pool_hbm, out_hbm, staged, in_sems, out_sems):
    pages = landed_hbm.shape[0]
    for page in range(pages):
        pltpu.make_async_copy(landed_hbm.at[page], staged.at[page], in_sems.at[page]).start()

    def each_target(page, begin):
        target = targets[page]

        @pl.when(target < pool_hbm.shape[0])
        def _():
            cp = pltpu.make_async_copy(staged.at[page], out_hbm.at[target], out_sems.at[page])
            cp.start() if begin else cp.wait()

    for page in range(pages):
        pltpu.make_async_copy(landed_hbm.at[page], staged.at[page], in_sems.at[page]).wait()
        each_target(page, True)
    for page in range(pages):
        each_target(page, False)


def write_pool(kv_pool, landed, targets):
    pages = landed.shape[0]
    return pl.pallas_call(
        pool_kernel,
        out_shape=jax.ShapeDtypeStruct(kv_pool.shape, kv_pool.dtype),
        grid_spec=pltpu.PrefetchScalarGridSpec(
            num_scalar_prefetch=1,
            grid=(1,),
            in_specs=[pl.BlockSpec(memory_space=pl.ANY), pl.BlockSpec(memory_space=pl.ANY)],
            out_specs=pl.BlockSpec(memory_space=pl.ANY),
            scratch_shapes=[
                pltpu.VMEM(landed.shape, landed.dtype),
                pltpu.SemaphoreType.DMA((pages,)),
                pltpu.SemaphoreType.DMA((pages,)),
            ],
        ),
        input_output_aliases={2: 0},
    )(targets.astype(jnp.int32), landed, kv_pool)


def copy_kernel(src_ref, dst_ref):
    dst_ref[...] = src_ref[...]


def copy_pool(kv_pool):
    pages = kv_pool.shape[0]
    block = (8,) + kv_pool.shape[1:]
    return pl.pallas_call(
        copy_kernel,
        out_shape=jax.ShapeDtypeStruct(kv_pool.shape, kv_pool.dtype),
        grid=(pages // 8,),
        in_specs=[pl.BlockSpec(block, lambda i: (i, 0, 0))],
        out_specs=pl.BlockSpec(block, lambda i: (i, 0, 0)),
    )(kv_pool)


def shards_body(queries, new_kv, kv_pool, window_table, append_table, cache_lengths):
    blocks = lax.axis_size("blk")
    groups = lax.axis_size("group")
    my_block = lax.axis_index("blk")
    piece_index = lax.axis_index("group")
    tok_rows = queries.shape[1]
    per_owner = kv_pool.shape[0]
    page_rows = kv_pool.shape[1]
    key_width = kv_pool.shape[2]
    head_size = key_width // 2
    head_count = queries.shape[2] // head_size
    win_pages = window_table.shape[1]
    new_pages = append_table.shape[1]
    win_rows = win_pages * page_rows
    cap_win = (win_pages + blocks - 1) // blocks
    cap_new = (new_pages + blocks - 1) // blocks
    piece_rows = page_rows // groups
    piece_start = piece_index * piece_rows
    fresh_keys = lax.all_gather(new_kv, "group", axis=1, tiled=True)[0]

    win_owner = window_table // per_owner
    win_rank = earlier_same(win_owner)
    win_wanted = (win_owner == my_block)[:, None, :] & (
        win_rank[:, None, :] == jnp.arange(cap_win)[None, :, None]
    )
    send_ids = pick_rows(win_wanted, window_table % per_owner)
    own_owner = lax.dynamic_index_in_dim(win_owner, my_block, 0, keepdims=False)
    own_rank = lax.dynamic_index_in_dim(win_rank, my_block, 0, keepdims=False)
    arrival = own_owner * cap_win + own_rank
    pool_piece = lax.dynamic_slice_in_dim(kv_pool, piece_start, piece_rows, axis=1)
    outgoing = pool_piece[send_ids.reshape(-1)]
    received = lax.all_to_all(outgoing, "blk", split_axis=0, concat_axis=0, tiled=True)
    pool_out = copy_pool(kv_pool)
    cached_piece = received[arrival]
    cached = lax.all_gather(cached_piece, "group", axis=1, tiled=True)

    new_owner = append_table // per_owner
    new_rank = earlier_same(new_owner)
    mine_owner = lax.dynamic_index_in_dim(new_owner, my_block, 0, keepdims=False)
    mine_rank = lax.dynamic_index_in_dim(new_rank, my_block, 0, keepdims=False)
    dest_wanted = (mine_owner[None, None, :] == jnp.arange(blocks)[:, None, None]) & (
        mine_rank[None, None, :] == jnp.arange(cap_new)[None, :, None]
    )
    page_pick = jnp.sum(jnp.where(dest_wanted, jnp.arange(new_pages)[None, None, :], 0), axis=2)
    fresh_pages = fresh_keys.reshape(new_pages, page_rows, key_width)
    fresh_piece = lax.dynamic_slice_in_dim(fresh_pages, piece_start, piece_rows, axis=1)
    parcels = fresh_piece[page_pick.reshape(-1)]
    arrived = lax.all_to_all(parcels, "blk", split_axis=0, concat_axis=0, tiled=True)
    land_here = new_owner == my_block
    land_source = jnp.argmax(land_here, axis=0)
    land_slot = land_source * cap_new + jnp.take_along_axis(new_rank, land_source[None, :], axis=0)[0]
    land_ids = jnp.take_along_axis(append_table % per_owner, land_source[None, :], axis=0)[0]
    land_live = jnp.any(land_here, axis=0)
    landed = lax.all_gather(arrived[land_slot], "group", axis=1, tiled=True)
    targets = jnp.where(land_live, land_ids, per_owner)
    new_pool = write_pool(pool_out, landed, targets)

    own_length = lax.dynamic_index_in_dim(cache_lengths, my_block, 0, keepdims=False)
    filled = jnp.minimum(own_length // page_rows, win_pages)
    first_row = piece_index * tok_rows
    live_from = (win_pages - filled) * page_rows - first_row
    attended = window_attention(
        queries[0], cached.reshape(win_rows, key_width), fresh_keys, piece_index, live_from,
        head_count, head_size, win_rows,
    )
    attn_out = attended.reshape(1, tok_rows, queries.shape[2])
    return (attn_out, new_pool)


def solution(mesh):
    in_specs = (
        P("blk", "group", None),
        P("blk", "group", None),
        P("blk", None, None),
        P(),
        P(),
        P(),
    )
    out_specs = (P("blk", "group", None), P("blk", None, None))
    return jax.shard_map(shards_body, mesh=mesh, in_specs=in_specs, out_specs=out_specs, check_vma=False)
```

```python
import functools

import jax
import jax.numpy as jnp
from jax import lax
from jax.experimental import pallas as pl
from jax.experimental.pallas import tpu as pltpu
from jax.sharding import Mesh, PartitionSpec as P


def earlier_same(owners):
    slot_count = owners.shape[1]
    same_owner = owners[:, :, None] == owners[:, None, :]
    before = jnp.arange(slot_count)[None, :] < jnp.arange(slot_count)[:, None]
    return jnp.sum(same_owner & before[None, :, :], axis=2)


def pick_rows(wanted, values):
    return jnp.sum(jnp.where(wanted, values[:, None, :], 0), axis=2)


def window_kernel(meta, q_ref, cached_hbm, fresh_hbm, out_ref, keys, bias, sems, *, chunk, chunks,
                  split, head_count, head_size, window_len):
    first = meta[0]
    live_from = meta[1]

    def chunk_copy(c, begin):
        j = first + c

        @pl.when(j < split)
        def _():
            cp = pltpu.make_async_copy(
                cached_hbm.at[pl.ds(j * chunk, chunk)], keys.at[pl.ds(c * chunk, chunk)], sems.at[c]
            )
            cp.start() if begin else cp.wait()

        @pl.when(j >= split)
        def _():
            cp = pltpu.make_async_copy(
                fresh_hbm.at[pl.ds((j - split) * chunk, chunk)], keys.at[pl.ds(c * chunk, chunk)], sems.at[c]
            )
            cp.start() if begin else cp.wait()

    for c in range(chunks):
        chunk_copy(c, True)
    rows = lax.broadcasted_iota(jnp.int32, bias.shape, 0)
    cols = lax.broadcasted_iota(jnp.int32, bias.shape, 1)
    allowed = (cols > rows) & (cols <= rows + window_len) & (cols >= live_from)
    bias[...] = jnp.where(allowed, 0.0, -jnp.inf).astype(jnp.float32)
    for c in range(chunks):
        chunk_copy(c, False)
    scale = head_size ** (-0.5)

    def one_head(h, carry):
        lanes = pl.ds(pl.multiple_of(h * head_size, head_size), head_size)
        scores = lax.dot_general(
            q_ref[:, lanes], keys[:, :head_size], (((1,), (1,)), ((), ())),
            preferred_element_type=jnp.float32,
        )
        scores = scores * scale + bias[...]
        row_max = jnp.max(scores, axis=1, keepdims=True)
        raw_weights = jnp.exp(scores - row_max)
        row_total = jnp.sum(raw_weights, axis=1, keepdims=True)
        weighted = jnp.dot(
            raw_weights.astype(jnp.bfloat16), keys[:, head_size:], preferred_element_type=jnp.float32
        )
        out_ref[:, lanes] = (weighted / row_total).astype(out_ref.dtype)
        return carry

    lax.fori_loop(0, head_count, one_head, 0)


def window_attention(query_rows, cached, fresh, first_chunk, live_from, head_count, head_size, window_len):
    tok_rows, width = query_rows.shape
    chunk = tok_rows
    span = window_len + tok_rows
    chunks = span // chunk
    split = cached.shape[0] // chunk
    key_width = cached.shape[1]
    body = functools.partial(
        window_kernel, chunk=chunk, chunks=chunks, split=split, head_count=head_count,
        head_size=head_size, window_len=window_len,
    )
    meta = jnp.stack([first_chunk, live_from]).astype(jnp.int32)
    return pl.pallas_call(
        body,
        out_shape=jax.ShapeDtypeStruct((tok_rows, width), query_rows.dtype),
        grid_spec=pltpu.PrefetchScalarGridSpec(
            num_scalar_prefetch=1,
            grid=(1,),
            in_specs=[
                pl.BlockSpec((tok_rows, width), lambda i, m: (0, 0)),
                pl.BlockSpec(memory_space=pl.ANY),
                pl.BlockSpec(memory_space=pl.ANY),
            ],
            out_specs=pl.BlockSpec((tok_rows, width), lambda i, m: (0, 0)),
            scratch_shapes=[
                pltpu.VMEM((span, key_width), cached.dtype),
                pltpu.VMEM((tok_rows, span), jnp.float32),
                pltpu.SemaphoreType.DMA((chunks,)),
            ],
        ),
        compiler_params=pltpu.CompilerParams(vmem_limit_bytes=48 * 1024 * 1024),
    )(meta, query_rows, cached, fresh)


def pool_kernel(targets, landed_hbm, pool_hbm, out_hbm, staged, in_sems, out_sems):
    pages = landed_hbm.shape[0]
    for page in range(pages):
        pltpu.make_async_copy(landed_hbm.at[page], staged.at[page], in_sems.at[page]).start()

    def each_target(page, begin):
        target = targets[page]

        @pl.when(target < pool_hbm.shape[0])
        def _():
            cp = pltpu.make_async_copy(staged.at[page], out_hbm.at[target], out_sems.at[page])
            cp.start() if begin else cp.wait()

    for page in range(pages):
        pltpu.make_async_copy(landed_hbm.at[page], staged.at[page], in_sems.at[page]).wait()
        each_target(page, True)
    for page in range(pages):
        each_target(page, False)


def write_pool(kv_pool, landed, targets):
    pages = landed.shape[0]
    return pl.pallas_call(
        pool_kernel,
        out_shape=jax.ShapeDtypeStruct(kv_pool.shape, kv_pool.dtype),
        grid_spec=pltpu.PrefetchScalarGridSpec(
            num_scalar_prefetch=1,
            grid=(1,),
            in_specs=[pl.BlockSpec(memory_space=pl.ANY), pl.BlockSpec(memory_space=pl.ANY)],
            out_specs=pl.BlockSpec(memory_space=pl.ANY),
            scratch_shapes=[
                pltpu.VMEM(landed.shape, landed.dtype),
                pltpu.SemaphoreType.DMA((pages,)),
                pltpu.SemaphoreType.DMA((pages,)),
            ],
        ),
        input_output_aliases={2: 0},
    )(targets.astype(jnp.int32), landed, kv_pool)


def copy_kernel(src_ref, dst_ref):
    dst_ref[...] = src_ref[...]


def copy_pool(kv_pool):
    pages = kv_pool.shape[0]
    block = (8,) + kv_pool.shape[1:]
    return pl.pallas_call(
        copy_kernel,
        out_shape=jax.ShapeDtypeStruct(kv_pool.shape, kv_pool.dtype),
        grid=(pages // 8,),
        in_specs=[pl.BlockSpec(block, lambda i: (i, 0, 0))],
        out_specs=pl.BlockSpec(block, lambda i: (i, 0, 0)),
    )(kv_pool)


def shards_body(queries, new_kv, kv_pool, window_table, append_table, cache_lengths):
    blocks = lax.axis_size("blk")
    groups = lax.axis_size("gx") * lax.axis_size("gc")
    my_block = lax.axis_index("blk")
    piece_index = lax.axis_index("gx") * lax.axis_size("gc") + lax.axis_index("gc")
    tok_rows = queries.shape[1]
    per_owner = kv_pool.shape[0]
    page_rows = kv_pool.shape[1]
    key_width = kv_pool.shape[2]
    head_size = key_width // 2
    head_count = queries.shape[2] // head_size
    win_pages = window_table.shape[1]
    new_pages = append_table.shape[1]
    win_rows = win_pages * page_rows
    cap_win = (win_pages + blocks - 1) // blocks
    cap_new = (new_pages + blocks - 1) // blocks
    piece_rows = page_rows // groups
    piece_start = piece_index * piece_rows
    fresh_keys = lax.all_gather(new_kv, ("gx", "gc"), axis=1, tiled=True)[0]

    win_owner = window_table // per_owner
    win_rank = earlier_same(win_owner)
    win_wanted = (win_owner == my_block)[:, None, :] & (
        win_rank[:, None, :] == jnp.arange(cap_win)[None, :, None]
    )
    send_ids = pick_rows(win_wanted, window_table % per_owner)
    own_owner = lax.dynamic_index_in_dim(win_owner, my_block, 0, keepdims=False)
    own_rank = lax.dynamic_index_in_dim(win_rank, my_block, 0, keepdims=False)
    arrival = own_owner * cap_win + own_rank
    pool_piece = lax.dynamic_slice_in_dim(kv_pool, piece_start, piece_rows, axis=1)
    outgoing = pool_piece[send_ids.reshape(-1)]
    received = lax.all_to_all(outgoing, "blk", split_axis=0, concat_axis=0, tiled=True)
    pool_out = copy_pool(kv_pool)
    cached_piece = received[arrival]
    cached = lax.all_gather(cached_piece, ("gx", "gc"), axis=1, tiled=True)

    new_owner = append_table // per_owner
    new_rank = earlier_same(new_owner)
    mine_owner = lax.dynamic_index_in_dim(new_owner, my_block, 0, keepdims=False)
    mine_rank = lax.dynamic_index_in_dim(new_rank, my_block, 0, keepdims=False)
    dest_wanted = (mine_owner[None, None, :] == jnp.arange(blocks)[:, None, None]) & (
        mine_rank[None, None, :] == jnp.arange(cap_new)[None, :, None]
    )
    page_pick = jnp.sum(jnp.where(dest_wanted, jnp.arange(new_pages)[None, None, :], 0), axis=2)
    fresh_pages = fresh_keys.reshape(new_pages, page_rows, key_width)
    fresh_piece = lax.dynamic_slice_in_dim(fresh_pages, piece_start, piece_rows, axis=1)
    parcels = fresh_piece[page_pick.reshape(-1)]
    arrived = lax.all_to_all(parcels, "blk", split_axis=0, concat_axis=0, tiled=True)
    land_here = new_owner == my_block
    land_source = jnp.argmax(land_here, axis=0)
    land_slot = land_source * cap_new + jnp.take_along_axis(new_rank, land_source[None, :], axis=0)[0]
    land_ids = jnp.take_along_axis(append_table % per_owner, land_source[None, :], axis=0)[0]
    land_live = jnp.any(land_here, axis=0)
    landed = lax.all_gather(arrived[land_slot], ("gx", "gc"), axis=1, tiled=True)
    targets = jnp.where(land_live, land_ids, per_owner)
    new_pool = write_pool(pool_out, landed, targets)

    own_length = lax.dynamic_index_in_dim(cache_lengths, my_block, 0, keepdims=False)
    filled = jnp.minimum(own_length // page_rows, win_pages)
    first_row = piece_index * tok_rows
    live_from = (win_pages - filled) * page_rows - first_row
    attended = window_attention(
        queries[0], cached.reshape(win_rows, key_width), fresh_keys, piece_index, live_from,
        head_count, head_size, win_rows,
    )
    attn_out = attended.reshape(1, tok_rows, queries.shape[2])
    return (attn_out, new_pool)


def solution(mesh):
    chip_count = mesh.shape["group"] // 2
    split = Mesh(mesh.devices.reshape(mesh.shape["blk"], chip_count, 2), ("blk", "gx", "gc"))
    tokens = ("gx", "gc")
    in_specs = (
        P("blk", tokens, None),
        P("blk", tokens, None),
        P("blk", None, None),
        P(),
        P(),
        P(),
    )
    out_specs = (P("blk", tokens, None), P("blk", None, None))
    return jax.shard_map(shards_body, mesh=split, in_specs=in_specs, out_specs=out_specs, check_vma=False)
```

```python
import functools

import jax
import jax.numpy as jnp
from jax import lax
from jax.experimental import pallas as pl
from jax.experimental.pallas import tpu as pltpu
from jax.sharding import PartitionSpec as P


def earlier_same(owners):
    slot_count = owners.shape[1]
    same_owner = owners[:, :, None] == owners[:, None, :]
    before = jnp.arange(slot_count)[None, :] < jnp.arange(slot_count)[:, None]
    return jnp.sum(same_owner & before[None, :, :], axis=2)


def pick_rows(wanted, values):
    return jnp.sum(jnp.where(wanted, values[:, None, :], 0), axis=2)


def window_kernel(meta, q_ref, cached_hbm, fresh_hbm, out_ref, keys, bias, sems, *, chunk, chunks,
                  split, head_count, head_size, window_len):
    first = meta[0]
    live_from = meta[1]

    def chunk_copy(c, begin):
        j = first + c

        @pl.when(j < split)
        def _():
            cp = pltpu.make_async_copy(
                cached_hbm.at[pl.ds(j * chunk, chunk)], keys.at[pl.ds(c * chunk, chunk)], sems.at[c]
            )
            cp.start() if begin else cp.wait()

        @pl.when(j >= split)
        def _():
            cp = pltpu.make_async_copy(
                fresh_hbm.at[pl.ds((j - split) * chunk, chunk)], keys.at[pl.ds(c * chunk, chunk)], sems.at[c]
            )
            cp.start() if begin else cp.wait()

    for c in range(chunks):
        chunk_copy(c, True)
    rows = lax.broadcasted_iota(jnp.int32, bias.shape, 0)
    cols = lax.broadcasted_iota(jnp.int32, bias.shape, 1)
    allowed = (cols > rows) & (cols <= rows + window_len) & (cols >= live_from)
    bias[...] = jnp.where(allowed, 0.0, -jnp.inf).astype(jnp.float32)
    for c in range(chunks):
        chunk_copy(c, False)
    scale = head_size ** (-0.5)

    def one_head(h, carry):
        lanes = pl.ds(pl.multiple_of(h * head_size, head_size), head_size)
        scores = lax.dot_general(
            q_ref[:, lanes], keys[:, :head_size], (((1,), (1,)), ((), ())),
            preferred_element_type=jnp.float32,
        )
        scores = scores * scale + bias[...]
        row_max = jnp.max(scores, axis=1, keepdims=True)
        raw_weights = jnp.exp(scores - row_max)
        row_total = jnp.sum(raw_weights, axis=1, keepdims=True)
        weighted = jnp.dot(
            raw_weights.astype(jnp.bfloat16), keys[:, head_size:], preferred_element_type=jnp.float32
        )
        out_ref[:, lanes] = (weighted / row_total).astype(out_ref.dtype)
        return carry

    lax.fori_loop(0, head_count, one_head, 0)


def window_attention(query_rows, cached, fresh, first_chunk, live_from, head_count, head_size, window_len):
    tok_rows, width = query_rows.shape
    chunk = tok_rows
    span = window_len + tok_rows
    chunks = span // chunk
    split = cached.shape[0] // chunk
    key_width = cached.shape[1]
    body = functools.partial(
        window_kernel, chunk=chunk, chunks=chunks, split=split, head_count=head_count,
        head_size=head_size, window_len=window_len,
    )
    meta = jnp.stack([first_chunk, live_from]).astype(jnp.int32)
    return pl.pallas_call(
        body,
        out_shape=jax.ShapeDtypeStruct((tok_rows, width), query_rows.dtype),
        grid_spec=pltpu.PrefetchScalarGridSpec(
            num_scalar_prefetch=1,
            grid=(1,),
            in_specs=[
                pl.BlockSpec((tok_rows, width), lambda i, m: (0, 0)),
                pl.BlockSpec(memory_space=pl.ANY),
                pl.BlockSpec(memory_space=pl.ANY),
            ],
            out_specs=pl.BlockSpec((tok_rows, width), lambda i, m: (0, 0)),
            scratch_shapes=[
                pltpu.VMEM((span, key_width), cached.dtype),
                pltpu.VMEM((tok_rows, span), jnp.float32),
                pltpu.SemaphoreType.DMA((chunks,)),
            ],
        ),
        compiler_params=pltpu.CompilerParams(vmem_limit_bytes=48 * 1024 * 1024),
    )(meta, query_rows, cached, fresh)


def pool_kernel(targets, landed_hbm, pool_hbm, out_hbm, staged, in_sems, out_sems):
    pages = landed_hbm.shape[0]
    for page in range(pages):
        pltpu.make_async_copy(landed_hbm.at[page], staged.at[page], in_sems.at[page]).start()

    def each_target(page, begin):
        target = targets[page]

        @pl.when(target < pool_hbm.shape[0])
        def _():
            cp = pltpu.make_async_copy(staged.at[page], out_hbm.at[target], out_sems.at[page])
            cp.start() if begin else cp.wait()

    for page in range(pages):
        pltpu.make_async_copy(landed_hbm.at[page], staged.at[page], in_sems.at[page]).wait()
        each_target(page, True)
    for page in range(pages):
        each_target(page, False)


def write_pool(kv_pool, landed, targets):
    pages = landed.shape[0]
    return pl.pallas_call(
        pool_kernel,
        out_shape=jax.ShapeDtypeStruct(kv_pool.shape, kv_pool.dtype),
        grid_spec=pltpu.PrefetchScalarGridSpec(
            num_scalar_prefetch=1,
            grid=(1,),
            in_specs=[pl.BlockSpec(memory_space=pl.ANY), pl.BlockSpec(memory_space=pl.ANY)],
            out_specs=pl.BlockSpec(memory_space=pl.ANY),
            scratch_shapes=[
                pltpu.VMEM(landed.shape, landed.dtype),
                pltpu.SemaphoreType.DMA((pages,)),
                pltpu.SemaphoreType.DMA((pages,)),
            ],
        ),
        input_output_aliases={2: 0},
    )(targets.astype(jnp.int32), landed, kv_pool)


def pick_kernel(slots, src_hbm, out_ref, sems):
    for row in range(out_ref.shape[0]):
        pltpu.make_async_copy(src_hbm.at[slots[row]], out_ref.at[row], sems.at[row]).start()
    for row in range(out_ref.shape[0]):
        pltpu.make_async_copy(src_hbm.at[slots[row]], out_ref.at[row], sems.at[row]).wait()


def pick_slots(slots_array, slots):
    count = slots.shape[0]
    shape = (count,) + slots_array.shape[1:]
    return pl.pallas_call(
        pick_kernel,
        out_shape=jax.ShapeDtypeStruct(shape, slots_array.dtype),
        grid_spec=pltpu.PrefetchScalarGridSpec(
            num_scalar_prefetch=1,
            grid=(1,),
            in_specs=[pl.BlockSpec(memory_space=pl.ANY)],
            out_specs=pl.BlockSpec(shape, lambda i, s: (0, 0, 0)),
            scratch_shapes=[pltpu.SemaphoreType.DMA((count,))],
        ),
    )(slots.astype(jnp.int32), slots_array)


def copy_kernel(src_ref, dst_ref):
    dst_ref[...] = src_ref[...]


def copy_pool(kv_pool):
    pages = kv_pool.shape[0]
    block = (8,) + kv_pool.shape[1:]
    return pl.pallas_call(
        copy_kernel,
        out_shape=jax.ShapeDtypeStruct(kv_pool.shape, kv_pool.dtype),
        grid=(pages // 8,),
        in_specs=[pl.BlockSpec(block, lambda i: (i, 0, 0))],
        out_specs=pl.BlockSpec(block, lambda i: (i, 0, 0)),
    )(kv_pool)


def shards_body(queries, new_kv, kv_pool, window_table, append_table, cache_lengths):
    blocks = lax.axis_size("blk")
    groups = lax.axis_size("group")
    my_block = lax.axis_index("blk")
    piece_index = lax.axis_index("group")
    tok_rows = queries.shape[1]
    per_owner = kv_pool.shape[0]
    page_rows = kv_pool.shape[1]
    key_width = kv_pool.shape[2]
    head_size = key_width // 2
    head_count = queries.shape[2] // head_size
    win_pages = window_table.shape[1]
    new_pages = append_table.shape[1]
    win_rows = win_pages * page_rows
    cap_win = (win_pages + blocks - 1) // blocks
    cap_new = (new_pages + blocks - 1) // blocks
    piece_rows = page_rows // groups
    piece_start = piece_index * piece_rows
    fresh_keys = lax.all_gather(new_kv, "group", axis=1, tiled=True)[0]

    win_owner = window_table // per_owner
    win_rank = earlier_same(win_owner)
    win_wanted = (win_owner == my_block)[:, None, :] & (
        win_rank[:, None, :] == jnp.arange(cap_win)[None, :, None]
    )
    send_ids = pick_rows(win_wanted, window_table % per_owner)
    own_owner = lax.dynamic_index_in_dim(win_owner, my_block, 0, keepdims=False)
    own_rank = lax.dynamic_index_in_dim(win_rank, my_block, 0, keepdims=False)
    arrival = own_owner * cap_win + own_rank
    pool_piece = lax.dynamic_slice_in_dim(kv_pool, piece_start, piece_rows, axis=1)
    outgoing = pool_piece[send_ids.reshape(-1)]
    received = lax.all_to_all(outgoing, "blk", split_axis=0, concat_axis=0, tiled=True)
    pool_out = copy_pool(kv_pool)
    cached_piece = pick_slots(received, arrival)
    cached = lax.all_gather(cached_piece, "group", axis=1, tiled=True)

    new_owner = append_table // per_owner
    new_rank = earlier_same(new_owner)
    mine_owner = lax.dynamic_index_in_dim(new_owner, my_block, 0, keepdims=False)
    mine_rank = lax.dynamic_index_in_dim(new_rank, my_block, 0, keepdims=False)
    dest_wanted = (mine_owner[None, None, :] == jnp.arange(blocks)[:, None, None]) & (
        mine_rank[None, None, :] == jnp.arange(cap_new)[None, :, None]
    )
    page_pick = jnp.sum(jnp.where(dest_wanted, jnp.arange(new_pages)[None, None, :], 0), axis=2)
    fresh_pages = fresh_keys.reshape(new_pages, page_rows, key_width)
    fresh_piece = lax.dynamic_slice_in_dim(fresh_pages, piece_start, piece_rows, axis=1)
    parcels = fresh_piece[page_pick.reshape(-1)]
    arrived = lax.all_to_all(parcels, "blk", split_axis=0, concat_axis=0, tiled=True)
    land_here = new_owner == my_block
    land_source = jnp.argmax(land_here, axis=0)
    land_slot = land_source * cap_new + jnp.take_along_axis(new_rank, land_source[None, :], axis=0)[0]
    land_ids = jnp.take_along_axis(append_table % per_owner, land_source[None, :], axis=0)[0]
    land_live = jnp.any(land_here, axis=0)
    landed = lax.all_gather(pick_slots(arrived, land_slot), "group", axis=1, tiled=True)
    targets = jnp.where(land_live, land_ids, per_owner)
    new_pool = write_pool(pool_out, landed, targets)

    own_length = lax.dynamic_index_in_dim(cache_lengths, my_block, 0, keepdims=False)
    filled = jnp.minimum(own_length // page_rows, win_pages)
    first_row = piece_index * tok_rows
    live_from = (win_pages - filled) * page_rows - first_row
    attended = window_attention(
        queries[0], cached.reshape(win_rows, key_width), fresh_keys, piece_index, live_from,
        head_count, head_size, win_rows,
    )
    attn_out = attended.reshape(1, tok_rows, queries.shape[2])
    return (attn_out, new_pool)


def solution(mesh):
    in_specs = (
        P("blk", "group", None),
        P("blk", "group", None),
        P("blk", None, None),
        P(),
        P(),
        P(),
    )
    out_specs = (P("blk", "group", None), P("blk", None, None))
    return jax.shard_map(shards_body, mesh=mesh, in_specs=in_specs, out_specs=out_specs, check_vma=False)
```

```python
import functools

import jax
import jax.numpy as jnp
from jax import lax
from jax.experimental import pallas as pl
from jax.experimental.pallas import tpu as pltpu
from jax.sharding import PartitionSpec as P


def earlier_same(owners):
    slot_count = owners.shape[1]
    same_owner = owners[:, :, None] == owners[:, None, :]
    before = jnp.arange(slot_count)[None, :] < jnp.arange(slot_count)[:, None]
    return jnp.sum(same_owner & before[None, :, :], axis=2)


def pick_rows(wanted, values):
    return jnp.sum(jnp.where(wanted, values[:, None, :], 0), axis=2)


def regroup(pieces):
    groups, pages, piece_rows, width = pieces.shape
    return pieces.transpose(1, 0, 2, 3).reshape(pages, groups * piece_rows, width)


def window_kernel(meta, q_ref, cached_hbm, fresh_hbm, out_ref, keys, bias, sems, *, chunk, chunks,
                  split, head_count, head_size, window_len):
    first = meta[0]
    live_from = meta[1]

    def chunk_copy(c, begin):
        j = first + c

        @pl.when(j < split)
        def _():
            cp = pltpu.make_async_copy(
                cached_hbm.at[pl.ds(j * chunk, chunk)], keys.at[pl.ds(c * chunk, chunk)], sems.at[c]
            )
            cp.start() if begin else cp.wait()

        @pl.when(j >= split)
        def _():
            cp = pltpu.make_async_copy(
                fresh_hbm.at[pl.ds((j - split) * chunk, chunk)], keys.at[pl.ds(c * chunk, chunk)], sems.at[c]
            )
            cp.start() if begin else cp.wait()

    for c in range(chunks):
        chunk_copy(c, True)
    rows = lax.broadcasted_iota(jnp.int32, bias.shape, 0)
    cols = lax.broadcasted_iota(jnp.int32, bias.shape, 1)
    allowed = (cols > rows) & (cols <= rows + window_len) & (cols >= live_from)
    bias[...] = jnp.where(allowed, 0.0, -jnp.inf).astype(jnp.float32)
    for c in range(chunks):
        chunk_copy(c, False)
    scale = head_size ** (-0.5)

    def one_head(h, carry):
        lanes = pl.ds(pl.multiple_of(h * head_size, head_size), head_size)
        scores = lax.dot_general(
            q_ref[:, lanes], keys[:, :head_size], (((1,), (1,)), ((), ())),
            preferred_element_type=jnp.float32,
        )
        scores = scores * scale + bias[...]
        row_max = jnp.max(scores, axis=1, keepdims=True)
        raw_weights = jnp.exp(scores - row_max)
        row_total = jnp.sum(raw_weights, axis=1, keepdims=True)
        weighted = jnp.dot(
            raw_weights.astype(jnp.bfloat16), keys[:, head_size:], preferred_element_type=jnp.float32
        )
        out_ref[:, lanes] = (weighted / row_total).astype(out_ref.dtype)
        return carry

    lax.fori_loop(0, head_count, one_head, 0)


def window_attention(query_rows, cached, fresh, first_chunk, live_from, head_count, head_size, window_len):
    tok_rows, width = query_rows.shape
    chunk = tok_rows
    span = window_len + tok_rows
    chunks = span // chunk
    split = cached.shape[0] // chunk
    key_width = cached.shape[1]
    body = functools.partial(
        window_kernel, chunk=chunk, chunks=chunks, split=split, head_count=head_count,
        head_size=head_size, window_len=window_len,
    )
    meta = jnp.stack([first_chunk, live_from]).astype(jnp.int32)
    return pl.pallas_call(
        body,
        out_shape=jax.ShapeDtypeStruct((tok_rows, width), query_rows.dtype),
        grid_spec=pltpu.PrefetchScalarGridSpec(
            num_scalar_prefetch=1,
            grid=(1,),
            in_specs=[
                pl.BlockSpec((tok_rows, width), lambda i, m: (0, 0)),
                pl.BlockSpec(memory_space=pl.ANY),
                pl.BlockSpec(memory_space=pl.ANY),
            ],
            out_specs=pl.BlockSpec((tok_rows, width), lambda i, m: (0, 0)),
            scratch_shapes=[
                pltpu.VMEM((span, key_width), cached.dtype),
                pltpu.VMEM((tok_rows, span), jnp.float32),
                pltpu.SemaphoreType.DMA((chunks,)),
            ],
        ),
        compiler_params=pltpu.CompilerParams(vmem_limit_bytes=48 * 1024 * 1024),
    )(meta, query_rows, cached, fresh)


def pool_kernel(targets, landed, pool_hbm, out_hbm, sems):
    groups, pages, piece_rows, _ = landed.shape
    for page in range(pages):
        target = targets[page]

        @pl.when(target < pool_hbm.shape[0])
        def _():
            for grp in range(groups):
                pltpu.make_async_copy(
                    landed.at[grp, page], out_hbm.at[target, pl.ds(grp * piece_rows, piece_rows)],
                    sems.at[page, grp],
                ).start()

    for page in range(pages):
        target = targets[page]

        @pl.when(target < pool_hbm.shape[0])
        def _():
            for grp in range(groups):
                pltpu.make_async_copy(
                    landed.at[grp, page], out_hbm.at[target, pl.ds(grp * piece_rows, piece_rows)],
                    sems.at[page, grp],
                ).wait()


def copy_kernel(src_ref, dst_ref):
    dst_ref[...] = src_ref[...]


def copy_pool(kv_pool):
    pages = kv_pool.shape[0]
    block = (8,) + kv_pool.shape[1:]
    return pl.pallas_call(
        copy_kernel,
        out_shape=jax.ShapeDtypeStruct(kv_pool.shape, kv_pool.dtype),
        grid=(pages // 8,),
        in_specs=[pl.BlockSpec(block, lambda i: (i, 0, 0))],
        out_specs=pl.BlockSpec(block, lambda i: (i, 0, 0)),
    )(kv_pool)


def write_pool(kv_pool, landed, targets):
    groups, pages = landed.shape[:2]
    return pl.pallas_call(
        pool_kernel,
        out_shape=jax.ShapeDtypeStruct(kv_pool.shape, kv_pool.dtype),
        grid_spec=pltpu.PrefetchScalarGridSpec(
            num_scalar_prefetch=1,
            grid=(1,),
            in_specs=[
                pl.BlockSpec(landed.shape, lambda i, t: (0, 0, 0, 0)),
                pl.BlockSpec(memory_space=pl.ANY),
            ],
            out_specs=pl.BlockSpec(memory_space=pl.ANY),
            scratch_shapes=[pltpu.SemaphoreType.DMA((pages, groups))],
        ),
        input_output_aliases={2: 0},
    )(targets.astype(jnp.int32), landed, kv_pool)


def shards_body(queries, new_kv, kv_pool, window_table, append_table, cache_lengths):
    blocks = lax.axis_size("blk")
    groups = lax.axis_size("group")
    my_block = lax.axis_index("blk")
    piece_index = lax.axis_index("group")
    tok_rows = queries.shape[1]
    per_owner = kv_pool.shape[0]
    page_rows = kv_pool.shape[1]
    key_width = kv_pool.shape[2]
    head_size = key_width // 2
    head_count = queries.shape[2] // head_size
    win_pages = window_table.shape[1]
    new_pages = append_table.shape[1]
    win_rows = win_pages * page_rows
    cap_win = (win_pages + blocks - 1) // blocks
    cap_new = (new_pages + blocks - 1) // blocks
    piece_rows = page_rows // groups
    piece_start = piece_index * piece_rows
    fresh_keys = lax.all_gather(new_kv, "group", axis=1, tiled=True)[0]

    win_owner = window_table // per_owner
    win_rank = earlier_same(win_owner)
    win_wanted = (win_owner == my_block)[:, None, :] & (
        win_rank[:, None, :] == jnp.arange(cap_win)[None, :, None]
    )
    send_ids = pick_rows(win_wanted, window_table % per_owner)
    own_owner = lax.dynamic_index_in_dim(win_owner, my_block, 0, keepdims=False)
    own_rank = lax.dynamic_index_in_dim(win_rank, my_block, 0, keepdims=False)
    arrival = own_owner * cap_win + own_rank
    pool_piece = lax.dynamic_slice_in_dim(kv_pool, piece_start, piece_rows, axis=1)
    outgoing = pool_piece[send_ids.reshape(-1)]
    received = lax.all_to_all(outgoing, "blk", split_axis=0, concat_axis=0, tiled=True)
    pool_out = copy_pool(kv_pool)
    cached_piece = received[arrival]
    cached = regroup(lax.all_gather(cached_piece, "group", axis=0, tiled=False))

    new_owner = append_table // per_owner
    new_rank = earlier_same(new_owner)
    mine_owner = lax.dynamic_index_in_dim(new_owner, my_block, 0, keepdims=False)
    mine_rank = lax.dynamic_index_in_dim(new_rank, my_block, 0, keepdims=False)
    dest_wanted = (mine_owner[None, None, :] == jnp.arange(blocks)[:, None, None]) & (
        mine_rank[None, None, :] == jnp.arange(cap_new)[None, :, None]
    )
    page_pick = jnp.sum(jnp.where(dest_wanted, jnp.arange(new_pages)[None, None, :], 0), axis=2)
    fresh_pages = fresh_keys.reshape(new_pages, page_rows, key_width)
    fresh_piece = lax.dynamic_slice_in_dim(fresh_pages, piece_start, piece_rows, axis=1)
    parcels = fresh_piece[page_pick.reshape(-1)]
    arrived = lax.all_to_all(parcels, "blk", split_axis=0, concat_axis=0, tiled=True)
    land_here = new_owner == my_block
    land_source = jnp.argmax(land_here, axis=0)
    land_slot = land_source * cap_new + jnp.take_along_axis(new_rank, land_source[None, :], axis=0)[0]
    land_ids = jnp.take_along_axis(append_table % per_owner, land_source[None, :], axis=0)[0]
    land_live = jnp.any(land_here, axis=0)
    landing = arrived[land_slot]
    targets = jnp.where(land_live, land_ids, per_owner)
    half = new_pages // 2
    new_pool = pool_out
    for lo, hi in ((0, half), (half, new_pages)):
        landed = lax.all_gather(landing[lo:hi], "group", axis=0, tiled=False)
        new_pool = write_pool(new_pool, landed, targets[lo:hi])

    own_length = lax.dynamic_index_in_dim(cache_lengths, my_block, 0, keepdims=False)
    filled = jnp.minimum(own_length // page_rows, win_pages)
    first_row = piece_index * tok_rows
    live_from = (win_pages - filled) * page_rows - first_row
    attended = window_attention(
        queries[0], cached.reshape(win_rows, key_width), fresh_keys, piece_index, live_from,
        head_count, head_size, win_rows,
    )
    attn_out = attended.reshape(1, tok_rows, queries.shape[2])
    return (attn_out, new_pool)


def solution(mesh):
    in_specs = (
        P("blk", "group", None),
        P("blk", "group", None),
        P("blk", None, None),
        P(),
        P(),
        P(),
    )
    out_specs = (P("blk", "group", None), P("blk", None, None))
    return jax.shard_map(shards_body, mesh=mesh, in_specs=in_specs, out_specs=out_specs, check_vma=False)
```

```python
import functools

import jax
import jax.numpy as jnp
from jax import lax
from jax.experimental import pallas as pl
from jax.experimental.pallas import tpu as pltpu
from jax.sharding import PartitionSpec as P


def earlier_same(owners):
    slot_count = owners.shape[1]
    same_owner = owners[:, :, None] == owners[:, None, :]
    before = jnp.arange(slot_count)[None, :] < jnp.arange(slot_count)[:, None]
    return jnp.sum(same_owner & before[None, :, :], axis=2)


def pick_rows(wanted, values):
    return jnp.sum(jnp.where(wanted, values[:, None, :], 0), axis=2)


def regroup(pieces):
    groups, pages, piece_rows, width = pieces.shape
    return pieces.transpose(1, 0, 2, 3).reshape(pages, groups * piece_rows, width)


def window_kernel(meta, q_ref, cached_hbm, fresh_hbm, out_ref, keys, bias, sems, *, chunk, chunks,
                  split, head_count, head_size, window_len):
    first = meta[0]
    live_from = meta[1]

    def chunk_copy(c, begin):
        j = first + c

        @pl.when(j < split)
        def _():
            cp = pltpu.make_async_copy(
                cached_hbm.at[pl.ds(j * chunk, chunk)], keys.at[pl.ds(c * chunk, chunk)], sems.at[c]
            )
            cp.start() if begin else cp.wait()

        @pl.when(j >= split)
        def _():
            cp = pltpu.make_async_copy(
                fresh_hbm.at[pl.ds((j - split) * chunk, chunk)], keys.at[pl.ds(c * chunk, chunk)], sems.at[c]
            )
            cp.start() if begin else cp.wait()

    for c in range(chunks):
        chunk_copy(c, True)
    rows = lax.broadcasted_iota(jnp.int32, bias.shape, 0)
    cols = lax.broadcasted_iota(jnp.int32, bias.shape, 1)
    allowed = (cols > rows) & (cols <= rows + window_len) & (cols >= live_from)
    bias[...] = jnp.where(allowed, 0.0, -jnp.inf).astype(jnp.float32)
    for c in range(chunks):
        chunk_copy(c, False)
    scale = head_size ** (-0.5)

    def one_head(h, carry):
        lanes = pl.ds(pl.multiple_of(h * head_size, head_size), head_size)
        scores = lax.dot_general(
            q_ref[:, lanes], keys[:, :head_size], (((1,), (1,)), ((), ())),
            preferred_element_type=jnp.float32,
        )
        scores = scores * scale + bias[...]
        row_max = jnp.max(scores, axis=1, keepdims=True)
        raw_weights = jnp.exp(scores - row_max)
        row_total = jnp.sum(raw_weights, axis=1, keepdims=True)
        weighted = jnp.dot(
            raw_weights.astype(jnp.bfloat16), keys[:, head_size:], preferred_element_type=jnp.float32
        )
        out_ref[:, lanes] = (weighted / row_total).astype(out_ref.dtype)
        return carry

    lax.fori_loop(0, head_count, one_head, 0)


def window_attention(query_rows, cached, fresh, first_chunk, live_from, head_count, head_size, window_len):
    tok_rows, width = query_rows.shape
    chunk = tok_rows
    span = window_len + tok_rows
    chunks = span // chunk
    split = cached.shape[0] // chunk
    key_width = cached.shape[1]
    body = functools.partial(
        window_kernel, chunk=chunk, chunks=chunks, split=split, head_count=head_count,
        head_size=head_size, window_len=window_len,
    )
    meta = jnp.stack([first_chunk, live_from]).astype(jnp.int32)
    return pl.pallas_call(
        body,
        out_shape=jax.ShapeDtypeStruct((tok_rows, width), query_rows.dtype),
        grid_spec=pltpu.PrefetchScalarGridSpec(
            num_scalar_prefetch=1,
            grid=(1,),
            in_specs=[
                pl.BlockSpec((tok_rows, width), lambda i, m: (0, 0)),
                pl.BlockSpec(memory_space=pl.ANY),
                pl.BlockSpec(memory_space=pl.ANY),
            ],
            out_specs=pl.BlockSpec((tok_rows, width), lambda i, m: (0, 0)),
            scratch_shapes=[
                pltpu.VMEM((span, key_width), cached.dtype),
                pltpu.VMEM((tok_rows, span), jnp.float32),
                pltpu.SemaphoreType.DMA((chunks,)),
            ],
        ),
        compiler_params=pltpu.CompilerParams(vmem_limit_bytes=48 * 1024 * 1024),
    )(meta, query_rows, cached, fresh)


def pool_kernel(targets, landed_hbm, pool_hbm, out_hbm, staged, in_sems, out_sems):
    pages = landed_hbm.shape[0]
    for page in range(pages):
        pltpu.make_async_copy(landed_hbm.at[page], staged.at[page], in_sems.at[page]).start()

    def each_target(page, begin):
        target = targets[page]

        @pl.when(target < pool_hbm.shape[0])
        def _():
            cp = pltpu.make_async_copy(staged.at[page], out_hbm.at[target], out_sems.at[page])
            cp.start() if begin else cp.wait()

    for page in range(pages):
        pltpu.make_async_copy(landed_hbm.at[page], staged.at[page], in_sems.at[page]).wait()
        each_target(page, True)
    for page in range(pages):
        each_target(page, False)


def write_pool(kv_pool, landed, targets):
    pages = landed.shape[0]
    return pl.pallas_call(
        pool_kernel,
        out_shape=jax.ShapeDtypeStruct(kv_pool.shape, kv_pool.dtype),
        grid_spec=pltpu.PrefetchScalarGridSpec(
            num_scalar_prefetch=1,
            grid=(1,),
            in_specs=[pl.BlockSpec(memory_space=pl.ANY), pl.BlockSpec(memory_space=pl.ANY)],
            out_specs=pl.BlockSpec(memory_space=pl.ANY),
            scratch_shapes=[
                pltpu.VMEM(landed.shape, landed.dtype),
                pltpu.SemaphoreType.DMA((pages,)),
                pltpu.SemaphoreType.DMA((pages,)),
            ],
        ),
        input_output_aliases={2: 0},
    )(targets.astype(jnp.int32), landed, kv_pool)


def copy_kernel(src_ref, dst_ref):
    dst_ref[...] = src_ref[...]


def copy_pool(kv_pool):
    pages = kv_pool.shape[0]
    block = (8,) + kv_pool.shape[1:]
    return pl.pallas_call(
        copy_kernel,
        out_shape=jax.ShapeDtypeStruct(kv_pool.shape, kv_pool.dtype),
        grid=(pages // 8,),
        in_specs=[pl.BlockSpec(block, lambda i: (i, 0, 0))],
        out_specs=pl.BlockSpec(block, lambda i: (i, 0, 0)),
    )(kv_pool)


def shards_body(queries, new_kv, kv_pool, window_table, append_table, cache_lengths):
    blocks = lax.axis_size("blk")
    groups = lax.axis_size("group")
    my_block = lax.axis_index("blk")
    piece_index = lax.axis_index("group")
    tok_rows = queries.shape[1]
    per_owner = kv_pool.shape[0]
    page_rows = kv_pool.shape[1]
    key_width = kv_pool.shape[2]
    head_size = key_width // 2
    head_count = queries.shape[2] // head_size
    win_pages = window_table.shape[1]
    new_pages = append_table.shape[1]
    win_rows = win_pages * page_rows
    cap_win = (win_pages + blocks - 1) // blocks
    cap_new = (new_pages + blocks - 1) // blocks
    piece_rows = page_rows // groups
    piece_start = piece_index * piece_rows
    fresh_keys = lax.all_gather(new_kv, "group", axis=1, tiled=True)[0]

    win_owner = window_table // per_owner
    win_rank = earlier_same(win_owner)
    win_wanted = (win_owner == my_block)[:, None, :] & (
        win_rank[:, None, :] == jnp.arange(cap_win)[None, :, None]
    )
    send_ids = pick_rows(win_wanted, window_table % per_owner)
    own_owner = lax.dynamic_index_in_dim(win_owner, my_block, 0, keepdims=False)
    own_rank = lax.dynamic_index_in_dim(win_rank, my_block, 0, keepdims=False)
    arrival = own_owner * cap_win + own_rank
    pool_piece = lax.dynamic_slice_in_dim(kv_pool, piece_start, piece_rows, axis=1)
    outgoing = pool_piece[send_ids.reshape(-1)]
    received = lax.all_to_all(outgoing, "blk", split_axis=0, concat_axis=0, tiled=True)
    pool_out = copy_pool(kv_pool)
    cached_piece = received[arrival]
    cached = regroup(lax.all_gather(cached_piece, "group", axis=0, tiled=False))

    new_owner = append_table // per_owner
    new_rank = earlier_same(new_owner)
    mine_owner = lax.dynamic_index_in_dim(new_owner, my_block, 0, keepdims=False)
    mine_rank = lax.dynamic_index_in_dim(new_rank, my_block, 0, keepdims=False)
    dest_wanted = (mine_owner[None, None, :] == jnp.arange(blocks)[:, None, None]) & (
        mine_rank[None, None, :] == jnp.arange(cap_new)[None, :, None]
    )
    page_pick = jnp.sum(jnp.where(dest_wanted, jnp.arange(new_pages)[None, None, :], 0), axis=2)
    fresh_pages = fresh_keys.reshape(new_pages, page_rows, key_width)
    fresh_piece = lax.dynamic_slice_in_dim(fresh_pages, piece_start, piece_rows, axis=1)
    parcels = fresh_piece[page_pick.reshape(-1)]
    arrived = lax.all_to_all(parcels, "blk", split_axis=0, concat_axis=0, tiled=True)
    land_here = new_owner == my_block
    land_source = jnp.argmax(land_here, axis=0)
    land_slot = land_source * cap_new + jnp.take_along_axis(new_rank, land_source[None, :], axis=0)[0]
    land_ids = jnp.take_along_axis(append_table % per_owner, land_source[None, :], axis=0)[0]
    land_live = jnp.any(land_here, axis=0)
    landed = lax.all_gather(arrived[land_slot], "group", axis=1, tiled=True)
    targets = jnp.where(land_live, land_ids, per_owner)
    new_pool = write_pool(pool_out, landed, targets)

    own_length = lax.dynamic_index_in_dim(cache_lengths, my_block, 0, keepdims=False)
    filled = jnp.minimum(own_length // page_rows, win_pages)
    first_row = piece_index * tok_rows
    live_from = (win_pages - filled) * page_rows - first_row
    attended = window_attention(
        queries[0], cached.reshape(win_rows, key_width), fresh_keys, piece_index, live_from,
        head_count, head_size, win_rows,
    )
    attn_out = attended.reshape(1, tok_rows, queries.shape[2])
    return (attn_out, new_pool)


def solution(mesh):
    in_specs = (
        P("blk", "group", None),
        P("blk", "group", None),
        P("blk", None, None),
        P(),
        P(),
        P(),
    )
    out_specs = (P("blk", "group", None), P("blk", None, None))
    return jax.shard_map(shards_body, mesh=mesh, in_specs=in_specs, out_specs=out_specs, check_vma=False)
```

```python
import functools

import jax
import jax.numpy as jnp
from jax import lax
from jax.experimental import pallas as pl
from jax.experimental.pallas import tpu as pltpu
from jax.sharding import PartitionSpec as P


def earlier_same(owners):
    slot_count = owners.shape[1]
    same_owner = owners[:, :, None] == owners[:, None, :]
    before = jnp.arange(slot_count)[None, :] < jnp.arange(slot_count)[:, None]
    return jnp.sum(same_owner & before[None, :, :], axis=2)


def pick_rows(wanted, values):
    return jnp.sum(jnp.where(wanted, values[:, None, :], 0), axis=2)


def regroup(pieces):
    groups, pages, piece_rows, width = pieces.shape
    return pieces.transpose(1, 0, 2, 3).reshape(pages, groups * piece_rows, width)


def window_kernel(meta, q_ref, cached_hbm, fresh_hbm, out_ref, keys, bias, sems, *, chunk, chunks,
                  split, head_count, head_size, window_len):
    first = meta[0]
    live_from = meta[1]

    def chunk_copy(c, begin):
        j = first + c

        @pl.when(j < split)
        def _():
            cp = pltpu.make_async_copy(
                cached_hbm.at[pl.ds(j * chunk, chunk)], keys.at[pl.ds(c * chunk, chunk)], sems.at[c]
            )
            cp.start() if begin else cp.wait()

        @pl.when(j >= split)
        def _():
            cp = pltpu.make_async_copy(
                fresh_hbm.at[pl.ds((j - split) * chunk, chunk)], keys.at[pl.ds(c * chunk, chunk)], sems.at[c]
            )
            cp.start() if begin else cp.wait()

    for c in range(chunks):
        chunk_copy(c, True)
    rows = lax.broadcasted_iota(jnp.int32, bias.shape, 0)
    cols = lax.broadcasted_iota(jnp.int32, bias.shape, 1)
    allowed = (cols > rows) & (cols <= rows + window_len) & (cols >= live_from)
    bias[...] = jnp.where(allowed, 0.0, -jnp.inf).astype(jnp.float32)
    for c in range(chunks):
        chunk_copy(c, False)
    scale = head_size ** (-0.5)

    def one_head(h, carry):
        lanes = pl.ds(pl.multiple_of(h * head_size, head_size), head_size)
        scores = lax.dot_general(
            q_ref[:, lanes], keys[:, :head_size], (((1,), (1,)), ((), ())),
            preferred_element_type=jnp.float32,
        )
        scores = scores * scale + bias[...]
        row_max = jnp.max(scores, axis=1, keepdims=True)
        raw_weights = jnp.exp(scores - row_max)
        row_total = jnp.sum(raw_weights, axis=1, keepdims=True)
        weighted = jnp.dot(
            raw_weights.astype(jnp.bfloat16), keys[:, head_size:], preferred_element_type=jnp.float32
        )
        out_ref[:, lanes] = (weighted / row_total).astype(out_ref.dtype)
        return carry

    lax.fori_loop(0, head_count, one_head, 0)


def window_attention(query_rows, cached, fresh, first_chunk, live_from, head_count, head_size, window_len):
    tok_rows, width = query_rows.shape
    chunk = tok_rows
    span = window_len + tok_rows
    chunks = span // chunk
    split = cached.shape[0] // chunk
    key_width = cached.shape[1]
    body = functools.partial(
        window_kernel, chunk=chunk, chunks=chunks, split=split, head_count=head_count,
        head_size=head_size, window_len=window_len,
    )
    meta = jnp.stack([first_chunk, live_from]).astype(jnp.int32)
    return pl.pallas_call(
        body,
        out_shape=jax.ShapeDtypeStruct((tok_rows, width), query_rows.dtype),
        grid_spec=pltpu.PrefetchScalarGridSpec(
            num_scalar_prefetch=1,
            grid=(1,),
            in_specs=[
                pl.BlockSpec((tok_rows, width), lambda i, m: (0, 0)),
                pl.BlockSpec(memory_space=pl.ANY),
                pl.BlockSpec(memory_space=pl.ANY),
            ],
            out_specs=pl.BlockSpec((tok_rows, width), lambda i, m: (0, 0)),
            scratch_shapes=[
                pltpu.VMEM((span, key_width), cached.dtype),
                pltpu.VMEM((tok_rows, span), jnp.float32),
                pltpu.SemaphoreType.DMA((chunks,)),
            ],
        ),
        compiler_params=pltpu.CompilerParams(vmem_limit_bytes=48 * 1024 * 1024),
    )(meta, query_rows, cached, fresh)


def pool_kernel(targets, landed_hbm, pool_hbm, out_hbm, staged, in_sems, out_sems):
    pages = landed_hbm.shape[0]
    ahead = min(4, pages)

    def fetch(page):
        return pltpu.make_async_copy(landed_hbm.at[page], staged.at[page], in_sems.at[page])

    def each_target(page, begin):
        target = targets[page]

        @pl.when(target < pool_hbm.shape[0])
        def _():
            cp = pltpu.make_async_copy(staged.at[page], out_hbm.at[target], out_sems.at[page])
            cp.start() if begin else cp.wait()

    for page in range(ahead):
        fetch(page).start()
    for page in range(pages):
        fetch(page).wait()
        each_target(page, True)
        if page + ahead < pages:
            fetch(page + ahead).start()
    for page in range(pages):
        each_target(page, False)


def write_pool(kv_pool, landed, targets):
    pages = landed.shape[0]
    return pl.pallas_call(
        pool_kernel,
        out_shape=jax.ShapeDtypeStruct(kv_pool.shape, kv_pool.dtype),
        grid_spec=pltpu.PrefetchScalarGridSpec(
            num_scalar_prefetch=1,
            grid=(1,),
            in_specs=[pl.BlockSpec(memory_space=pl.ANY), pl.BlockSpec(memory_space=pl.ANY)],
            out_specs=pl.BlockSpec(memory_space=pl.ANY),
            scratch_shapes=[
                pltpu.VMEM(landed.shape, landed.dtype),
                pltpu.SemaphoreType.DMA((pages,)),
                pltpu.SemaphoreType.DMA((pages,)),
            ],
        ),
        input_output_aliases={2: 0},
    )(targets.astype(jnp.int32), landed, kv_pool)


def copy_kernel(src_ref, dst_ref):
    dst_ref[...] = src_ref[...]


def copy_pool(kv_pool):
    pages = kv_pool.shape[0]
    block = (8,) + kv_pool.shape[1:]
    return pl.pallas_call(
        copy_kernel,
        out_shape=jax.ShapeDtypeStruct(kv_pool.shape, kv_pool.dtype),
        grid=(pages // 8,),
        in_specs=[pl.BlockSpec(block, lambda i: (i, 0, 0))],
        out_specs=pl.BlockSpec(block, lambda i: (i, 0, 0)),
    )(kv_pool)


def shards_body(queries, new_kv, kv_pool, window_table, append_table, cache_lengths):
    blocks = lax.axis_size("blk")
    groups = lax.axis_size("group")
    my_block = lax.axis_index("blk")
    piece_index = lax.axis_index("group")
    tok_rows = queries.shape[1]
    per_owner = kv_pool.shape[0]
    page_rows = kv_pool.shape[1]
    key_width = kv_pool.shape[2]
    head_size = key_width // 2
    head_count = queries.shape[2] // head_size
    win_pages = window_table.shape[1]
    new_pages = append_table.shape[1]
    win_rows = win_pages * page_rows
    cap_win = (win_pages + blocks - 1) // blocks
    cap_new = (new_pages + blocks - 1) // blocks
    piece_rows = page_rows // groups
    piece_start = piece_index * piece_rows
    fresh_keys = lax.all_gather(new_kv, "group", axis=1, tiled=True)[0]

    win_owner = window_table // per_owner
    win_rank = earlier_same(win_owner)
    win_wanted = (win_owner == my_block)[:, None, :] & (
        win_rank[:, None, :] == jnp.arange(cap_win)[None, :, None]
    )
    send_ids = pick_rows(win_wanted, window_table % per_owner)
    own_owner = lax.dynamic_index_in_dim(win_owner, my_block, 0, keepdims=False)
    own_rank = lax.dynamic_index_in_dim(win_rank, my_block, 0, keepdims=False)
    arrival = own_owner * cap_win + own_rank
    pool_piece = lax.dynamic_slice_in_dim(kv_pool, piece_start, piece_rows, axis=1)
    outgoing = pool_piece[send_ids.reshape(-1)]
    received = lax.all_to_all(outgoing, "blk", split_axis=0, concat_axis=0, tiled=True)
    pool_out = copy_pool(kv_pool)
    cached_piece = received[arrival]
    cached = regroup(lax.all_gather(cached_piece, "group", axis=0, tiled=False))

    new_owner = append_table // per_owner
    new_rank = earlier_same(new_owner)
    mine_owner = lax.dynamic_index_in_dim(new_owner, my_block, 0, keepdims=False)
    mine_rank = lax.dynamic_index_in_dim(new_rank, my_block, 0, keepdims=False)
    dest_wanted = (mine_owner[None, None, :] == jnp.arange(blocks)[:, None, None]) & (
        mine_rank[None, None, :] == jnp.arange(cap_new)[None, :, None]
    )
    page_pick = jnp.sum(jnp.where(dest_wanted, jnp.arange(new_pages)[None, None, :], 0), axis=2)
    fresh_pages = fresh_keys.reshape(new_pages, page_rows, key_width)
    fresh_piece = lax.dynamic_slice_in_dim(fresh_pages, piece_start, piece_rows, axis=1)
    parcels = fresh_piece[page_pick.reshape(-1)]
    arrived = lax.all_to_all(parcels, "blk", split_axis=0, concat_axis=0, tiled=True)
    land_here = new_owner == my_block
    land_source = jnp.argmax(land_here, axis=0)
    land_slot = land_source * cap_new + jnp.take_along_axis(new_rank, land_source[None, :], axis=0)[0]
    land_ids = jnp.take_along_axis(append_table % per_owner, land_source[None, :], axis=0)[0]
    land_live = jnp.any(land_here, axis=0)
    landed = lax.all_gather(arrived[land_slot], "group", axis=1, tiled=True)
    targets = jnp.where(land_live, land_ids, per_owner)
    new_pool = write_pool(pool_out, landed, targets)

    own_length = lax.dynamic_index_in_dim(cache_lengths, my_block, 0, keepdims=False)
    filled = jnp.minimum(own_length // page_rows, win_pages)
    first_row = piece_index * tok_rows
    live_from = (win_pages - filled) * page_rows - first_row
    attended = window_attention(
        queries[0], cached.reshape(win_rows, key_width), fresh_keys, piece_index, live_from,
        head_count, head_size, win_rows,
    )
    attn_out = attended.reshape(1, tok_rows, queries.shape[2])
    return (attn_out, new_pool)


def solution(mesh):
    in_specs = (
        P("blk", "group", None),
        P("blk", "group", None),
        P("blk", None, None),
        P(),
        P(),
        P(),
    )
    out_specs = (P("blk", "group", None), P("blk", None, None))
    return jax.shard_map(shards_body, mesh=mesh, in_specs=in_specs, out_specs=out_specs, check_vma=False)
```
